256 devices in a mesh: gx: 2 (over core), gy: 32 (over z, x), gz: 4 (over y).
Axes of the slice: x: 4, y: 4, z: 8, core: 2. Of those that a mesh axis runs over, the one named last changes fastest.
Arguments:
- point_values: float32 [3, 64, 1048576], P(None, None, ('gx', 'gy', 'gz')), may hold values from -6 to 6
- owner: int32 [1048576], P(('gx', 'gy', 'gz')), may hold values from 0 to 63, as said below
- slot: int32 [1048576], P(('gx', 'gy', 'gz')), may hold values from 0 to 2047, as said below
- live_count: int32 [256], P(('gx', 'gy', 'gz')), may hold values from 0 to 4096, as said below
Outputs:
- coeffs: float32 [3, 64, 1024, 512], P(None, 'gx', 'gy', 'gz')
The draws below stay inside these ranges and needn't reach their ends.
Inputs may be any that keep to these rules, and one draw needn't show every extreme that they name: `owner`: within each layer of bricks along z (devices with one gz index), every place of every brick is named by exactly one live slot of that layer's devices; values of dead slots are arbitrary. `slot`: the live slots of one source device name at most 64 elements of one brick; in every layer some device names exactly 64 for every brick. `live_count`: in every layer some device has 4096 live slots; the live slots are the first ones of a device.
All inputs are finite; a program needn't handle non-finite values.
Results may differ from the reference program's by a relative error of at most 0.00011.
Values sent between devices are 32-bit elements; how exact they have to be, the bound alone decides.
No kernel may reach another device: no remote copies, remote signals or barrier semaphores. Data moves between devices by JAX's collectives and lax.ppermute only.
A program may use at most 192 MiB of HBM per device.

```python
import jax
import jax.numpy as jnp
import numpy as np
from jax import lax

BX = 32
BY = 32
BZ = 128
LEVELS = 3
FIELDS = 3
POINTS = 64
ELEM_DEV = 2048
CAP = 4096
SLAB = 64
LAYERS = 4
SLOTS = 1048576
N_GX = 2
N_GY = 32
N_GZ = 4


def one_layer(layer_key):
    base_quota = ELEM_DEV // SLAB
    key_level, key_share, key_perm, key_order, key_owner, key_slot = jax.random.split(layer_key, 6)
    levels = jax.random.randint(key_level, (SLAB,), 0, 5)
    share = jax.random.randint(key_share, (SLAB, SLAB), 0, base_quota + 1) * levels[:, None] // 4
    share = share.at[0].set(base_quota).at[1].set(0)
    sends = base_quota + share - jnp.roll(share, -1, axis=0)
    totals = jnp.sum(sends, axis=1)
    ends = jnp.cumsum(sends, axis=0)
    places = jnp.arange(ELEM_DEV, dtype=jnp.int32)
    source_of = jax.vmap(lambda column: jnp.searchsorted(column, places, side='right'))(ends.T).astype(jnp.int32)
    perms = jax.vmap(lambda perm_key: jax.random.permutation(perm_key, ELEM_DEV))(jax.random.split(key_perm, SLAB))
    flat_source = source_of.reshape(-1)
    flat_owner = jnp.repeat(jnp.arange(SLAB, dtype=jnp.int32), ELEM_DEV)
    flat_slot = perms.reshape(-1).astype(jnp.int32)
    shuffle = jax.random.permutation(key_order, SLAB * ELEM_DEV).astype(jnp.int32)
    order = jnp.argsort(flat_source * (SLAB * ELEM_DEV) + shuffle)
    sorted_source = flat_source[order]
    starts = jnp.cumsum(totals) - totals
    within = jnp.arange(SLAB * ELEM_DEV, dtype=jnp.int32) - starts[sorted_source]
    target_index = sorted_source * CAP + within
    owners = jax.random.randint(key_owner, (SLAB * CAP,), 0, SLAB).at[target_index].set(flat_owner[order])
    slots = jax.random.randint(key_slot, (SLAB * CAP,), 0, ELEM_DEV).at[target_index].set(flat_slot[order])
    return (owners.reshape(SLAB, CAP), slots.reshape(SLAB, CAP), totals.astype(jnp.int32))


def layout_tables(key):
    layer_keys = jax.random.split(jax.random.fold_in(key, 11), LAYERS)
    owners, slots, totals = jax.vmap(one_layer)(layer_keys)
    owners = owners.transpose(1, 0, 2).reshape(-1).astype(jnp.int32)
    slots = slots.transpose(1, 0, 2).reshape(-1).astype(jnp.int32)
    totals = totals.transpose(1, 0).reshape(-1).astype(jnp.int32)
    return (owners, slots, totals)


def draw_owner(key, part):
    return layout_tables(key)[0]


def draw_slot(key, part):
    return layout_tables(key)[1]


def draw_live_count(key, part):
    return layout_tables(key)[2]


def block_scale(stream_key, extent, cuts, smallest, largest):
    factor_of = 1.0
    for axis_at, shards_of in cuts:
        heights = jax.random.uniform(jax.random.fold_in(jax.random.fold_in(stream_key, 6), axis_at), (shards_of,), jnp.float32, smallest / len(cuts), largest / len(cuts))
        factor_of = factor_of * jnp.repeat(jnp.exp(heights), extent[axis_at] // shards_of).reshape((-1,) + (1,) * (len(extent) - 1 - axis_at))
    return factor_of


def normal_values(own_key, extent, scale, most, pieces=(), kind=jnp.bfloat16):
    factor_of = block_scale(own_key, extent, pieces, -0.22, 0.18) if pieces else 1.0
    values = jax.random.normal(own_key, extent, jnp.float32) * scale * factor_of
    return jnp.minimum(jnp.maximum(values, -most), most).astype(kind)


def setup_inputs(seed: int = 0) -> dict:
    splits = jax.random.split(jax.random.key(seed), 5)
    point_values = normal_values(splits[0], (FIELDS, POINTS, SLOTS), 1.0, 6.0, ((2, 256),), jnp.float32)
    owner = draw_owner(jax.random.fold_in(splits[4], 71), 0)
    slot = draw_slot(jax.random.fold_in(splits[4], 71), 0)
    live_count = draw_live_count(jax.random.fold_in(splits[4], 71), 0)
    return {"point_values": point_values, "owner": owner, "slot": slot, "live_count": live_count}


LIFT_A = -1.586134342
LIFT_B = -0.05298011854
LIFT_C = 0.8829110762
LIFT_D = 0.4435068522
LIFT_K = 1.149604398


def interpolation_matrix():
    nodes = np.array([-0.8611363116, -0.3399810436, 0.3399810436, 0.8611363116])
    targets = -0.75 + 0.5 * np.arange(4)
    table = np.ones((4, 4))
    for target_row in range(4):
        for node_col in range(4):
            for node_other in range(4):
                if node_other != node_col:
                    table[target_row, node_col] *= (targets[target_row] - nodes[node_other]) / (nodes[node_col] - nodes[node_other])
    full_table = (table[:, None, None, :, None, None] * table[None, :, None, None, :, None] * table[None, None, :, None, None, :]).reshape(64, 64)
    return jnp.asarray(full_table, dtype=jnp.float32)


def lift_periodic(signal, axis_dim):
    length = signal.shape[axis_dim]
    even_part = lax.slice_in_dim(signal, 0, length, 2, axis_dim)
    odd_part = lax.slice_in_dim(signal, 1, length, 2, axis_dim)
    odd_one = odd_part + LIFT_A * (even_part + jnp.roll(even_part, -1, axis_dim))
    even_two = even_part + LIFT_B * (jnp.roll(odd_one, 1, axis_dim) + odd_one)
    odd_three = odd_one + LIFT_C * (even_two + jnp.roll(even_two, -1, axis_dim))
    even_four = even_two + LIFT_D * (jnp.roll(odd_three, 1, axis_dim) + odd_three)
    return even_four / LIFT_K, odd_three * LIFT_K


def arrange_bricks(low_part, high_part, axis_dim, bricks):
    shape_now = low_part.shape
    split_shape = shape_now[:axis_dim] + (bricks, shape_now[axis_dim] // bricks) + shape_now[axis_dim + 1:]
    joined = jnp.concatenate([low_part.reshape(split_shape), high_part.reshape(split_shape)], axis_dim + 1)
    return joined.reshape(shape_now[:axis_dim] + (2 * shape_now[axis_dim],) + shape_now[axis_dim + 1:])


def build_grid(values, owner, slot, live_count):
    slots_all = owner.shape[0]
    index_all = jnp.arange(slots_all, dtype=jnp.int32)
    source = (index_all // CAP).astype(jnp.int32)
    live = (index_all % CAP) < live_count[source]
    layer = source % N_GZ
    brick_x = owner // N_GY
    brick_y = owner % N_GY
    elems_x = BX // 4
    elems_y = BY // 4
    elems_z = BZ // 4
    elem_x = slot // (elems_y * elems_z)
    elem_y = (slot // elems_z) % elems_y
    elem_z = slot % elems_z
    total_x = elems_x * N_GX
    total_y = elems_y * N_GY
    total_z = elems_z * N_GZ
    flat = ((brick_x * elems_x + elem_x) * total_y + brick_y * elems_y + elem_y) * total_z + layer * elems_z + elem_z
    flat = jnp.where(live, flat, total_x * total_y * total_z).astype(jnp.int32)
    placed = jnp.zeros((64, total_x * total_y * total_z), jnp.float32).at[:, flat].set(values, mode="drop")
    cells = placed.reshape(4, 4, 4, total_x, total_y, total_z).transpose(3, 0, 4, 1, 5, 2)
    return cells.reshape(total_x * 4, total_y * 4, total_z * 4)


def transform_field(grid):
    for level_index in range(LEVELS):
        size_x = BX >> level_index
        size_y = BY >> level_index
        size_z = BZ >> level_index
        blocks = grid.reshape(N_GX, BX, N_GY, BY, N_GZ, BZ)
        band = blocks[:, :size_x, :, :size_y, :, :size_z].reshape(N_GX * size_x, N_GY * size_y, N_GZ * size_z)
        low_part, high_part = lift_periodic(band, 0)
        band = arrange_bricks(low_part, high_part, 0, N_GX)
        low_part, high_part = lift_periodic(band, 1)
        band = arrange_bricks(low_part, high_part, 1, N_GY)
        low_part, high_part = lift_periodic(band, 2)
        band = arrange_bricks(low_part, high_part, 2, N_GZ)
        blocks = blocks.at[:, :size_x, :, :size_y, :, :size_z].set(band.reshape(N_GX, size_x, N_GY, size_y, N_GZ, size_z))
        grid = blocks.reshape(N_GX * BX, N_GY * BY, N_GZ * BZ)
    return grid


def reference(point_values, owner, slot, live_count):
    matrix = interpolation_matrix()
    results = []
    for field_index in range(FIELDS):
        uniform = jnp.dot(matrix, point_values[field_index], precision=lax.Precision.HIGHEST)
        grid = build_grid(uniform, owner, slot, live_count)
        results.append(transform_field(grid))
    return jnp.stack(results, axis=0)
```

```python
import jax
import jax.numpy as jnp
import numpy as np
from jax import lax
from jax.sharding import PartitionSpec as P

BX = 32
BY = 32
BZ = 128
LEVELS = 3


LIFT_A = -1.586134342
LIFT_B = -0.05298011854
LIFT_C = 0.8829110762
LIFT_D = 0.4435068522
LIFT_K = 1.149604398


def extended_2(cells, sides, width):
    for axis, dim in sides:
        count = lax.axis_size(axis)
        head = lax.slice_in_dim(cells, 0, width, axis=dim)
        tail = lax.slice_in_dim(cells, cells.shape[dim] - width, cells.shape[dim], axis=dim)
        cells = jnp.concatenate(
            [
                lax.ppermute(tail, axis, [(i, (i + 1) % count) for i in range(count)]),
                cells,
                lax.ppermute(head, axis, [((i + 1) % count, i) for i in range(count)]),
            ],
            axis=dim,
        )
    return cells


def interpolation_matrix():
    nodes = np.array([-0.8611363116, -0.3399810436, 0.3399810436, 0.8611363116])
    targets = -0.75 + 0.5 * np.arange(4)
    table = np.ones((4, 4))
    for target_row in range(4):
        for node_col in range(4):
            for node_other in range(4):
                if node_other != node_col:
                    table[target_row, node_col] *= (targets[target_row] - nodes[node_other]) / (
                        nodes[node_col] - nodes[node_other]
                    )
    full_table = (
        table[:, None, None, :, None, None]
        * table[None, :, None, None, :, None]
        * table[None, None, :, None, None, :]
    ).reshape(64, 64)
    return jnp.asarray(full_table, dtype=jnp.float32)


def lift_table(length):
    extended = np.eye(length + 8)
    half_count = length // 2 + 4
    even_part = extended[0::2]
    odd_part = extended[1::2]
    odd_one = odd_part[0 : half_count - 1] + LIFT_A * (
        even_part[0 : half_count - 1] + even_part[1:half_count]
    )
    even_two = even_part[1 : half_count - 1] + LIFT_B * (
        odd_one[0 : half_count - 2] + odd_one[1 : half_count - 1]
    )
    odd_three = odd_one[1 : half_count - 2] + LIFT_C * (
        even_two[0 : half_count - 3] + even_two[1 : half_count - 2]
    )
    even_four = even_two[1 : half_count - 3] + LIFT_D * (
        odd_three[0 : half_count - 4] + odd_three[1 : half_count - 3]
    )
    joined = np.concatenate([even_four / LIFT_K, odd_three[1 : length // 2 + 1] * LIFT_K], 0)
    return jnp.asarray(joined, dtype=jnp.float32)


def apply_points(values, matrix):
    return jnp.einsum("qp,fpe->fqe", matrix, values, precision=lax.Precision.HIGHEST)


def to_cells(elements, size_x, size_y, size_z):
    blocks = elements.reshape(3, 4, 4, 4, size_x // 4, size_y // 4, size_z // 4)
    return blocks.transpose(0, 4, 1, 5, 2, 6, 3).reshape(3, size_x, size_y, size_z)


def lift_axis(extended, axis_dim, length):
    table = lift_table(length)
    if axis_dim == 1:
        return jnp.einsum("ab,fbyz->fayz", table, extended, precision=lax.Precision.HIGHEST)
    if axis_dim == 2:
        return jnp.einsum("ab,fxbz->fxaz", table, extended, precision=lax.Precision.HIGHEST)
    return jnp.einsum("fxyb,ab->fxya", extended, table, precision=lax.Precision.HIGHEST)


def spread_table():
    table = np.zeros((32, 4, 128), np.float32)
    for z_index in range(32):
        for c_index in range(4):
            table[z_index, c_index, 4 * z_index + c_index] = 1.0
    return jnp.asarray(table)


def rank_in_owner(target, groups):
    slots_here = target.shape[0]
    block = 128
    blocks = slots_here // block
    owner_ids = jnp.arange(groups, dtype=jnp.int32)
    onehot = (target[None, :] == owner_ids[:, None]).astype(jnp.bfloat16)
    onehot = onehot.reshape(groups, blocks, block)
    upper = (jnp.arange(block)[:, None] < jnp.arange(block)[None, :]).astype(jnp.bfloat16)
    within = jnp.einsum("obk,kj->obj", onehot, upper, preferred_element_type=jnp.float32)
    totals = jnp.sum(onehot.astype(jnp.float32), axis=2)
    block_upper = (jnp.arange(blocks)[:, None] < jnp.arange(blocks)[None, :]).astype(jnp.float32)
    offsets = jnp.dot(totals, block_upper, precision=lax.Precision.HIGHEST)
    counts = within + offsets[:, :, None]
    rank = jnp.sum(onehot.astype(jnp.float32) * counts, axis=0)
    return rank.reshape(slots_here).astype(jnp.int32)


def on_device(point_values, owner, slot, live_count):
    rows_x = lax.axis_size("gx")
    rows_y = lax.axis_size("gy")
    slab_size = rows_x * rows_y
    brick_elems = BX * BY * BZ // 64
    pair_capacity = 2 * brick_elems // slab_size
    slots_here = owner.shape[0]
    width = slab_size * pair_capacity
    flat_values = point_values.reshape(3 * 64, slots_here)
    position = jnp.arange(slots_here, dtype=jnp.int32)
    live = position < live_count[0]
    target = jnp.where(live, owner, slab_size)
    rank = rank_in_owner(target, slab_size)
    column = jnp.where(live, target * pair_capacity + rank, width)
    payload = jnp.concatenate([flat_values, (slot + 1).astype(jnp.float32)[None, :]], axis=0)
    send = jnp.zeros((3 * 64 + 1, width), jnp.float32).at[:, column].set(payload, mode="drop")
    recv = lax.all_to_all(send, ("gx", "gy"), split_axis=1, concat_axis=1, tiled=True)
    marks = recv[3 * 64].astype(jnp.int32)
    recv_slots = jnp.where(marks > 0, marks - 1, brick_elems)
    placed = (
        jnp.zeros((3 * 64, brick_elems), jnp.float32)
        .at[:, recv_slots]
        .set(recv[: 3 * 64], mode="drop")
    )
    matrix = interpolation_matrix()
    elements = jnp.einsum(
        "qp,fpe->fqe", matrix, placed.reshape(3, 64, brick_elems), precision=lax.Precision.HIGHEST
    )
    blocks = elements.reshape(3, 4, 4, 4, BX // 4, BY // 4, BZ // 4)
    coeffs = jnp.einsum(
        "fabcxyz,zcw->fxaybw", blocks, spread_table(), precision=lax.Precision.HIGHEST
    ).reshape(3, BX, BY, BZ)
    for level_index in range(LEVELS):
        size_x = BX >> level_index
        size_y = BY >> level_index
        size_z = BZ >> level_index
        band = coeffs[:, :size_x, :size_y, :size_z]
        widened = extended_2(band, (("gx", 1),), 4)
        band = lift_axis(widened, 1, size_x)
        widened = extended_2(band, (("gy", 2),), 4)
        band = lift_axis(widened, 2, size_y)
        widened = extended_2(band, (("gz", 3),), 4)
        band = lift_axis(widened, 3, size_z)
        coeffs = coeffs.at[:, :size_x, :size_y, :size_z].set(band)
    return coeffs


def solution(mesh):
    in_specs = (
        P(None, None, ("gx", "gy", "gz")),
        P(("gx", "gy", "gz")),
        P(("gx", "gy", "gz")),
        P(("gx", "gy", "gz")),
    )
    out_specs = P(None, "gx", "gy", "gz")
    return jax.shard_map(
        on_device, mesh=mesh, in_specs=in_specs, out_specs=out_specs, check_vma=False
    )
```

```python
import jax
import jax.numpy as jnp
import numpy as np
from jax import lax
from jax.sharding import PartitionSpec as P

BX = 32
BY = 32
BZ = 128
LEVELS = 3


LIFT_A = -1.586134342
LIFT_B = -0.05298011854
LIFT_C = 0.8829110762
LIFT_D = 0.4435068522
LIFT_K = 1.149604398


def extended_2(cells, sides, width):
    for axis, dim in sides:
        count = lax.axis_size(axis)
        head = lax.slice_in_dim(cells, 0, width, axis=dim)
        tail = lax.slice_in_dim(cells, cells.shape[dim] - width, cells.shape[dim], axis=dim)
        cells = jnp.concatenate(
            [
                lax.ppermute(tail, axis, [(i, (i + 1) % count) for i in range(count)]),
                cells,
                lax.ppermute(head, axis, [((i + 1) % count, i) for i in range(count)]),
            ],
            axis=dim,
        )
    return cells


def halo_pieces(band, width):
    n_x = lax.axis_size("gx")
    n_y = lax.axis_size("gy")
    n_z = lax.axis_size("gz")
    axes = ("gx", "gy", "gz")

    def part(cells, dim, step):
        size = cells.shape[dim]
        if step < 0:
            return lax.slice_in_dim(cells, size - width, size, axis=dim)
        if step > 0:
            return lax.slice_in_dim(cells, 0, width, axis=dim)
        return cells

    def fetch(piece, step_x, step_y, step_z):
        pairs = []
        for x_at in range(n_x):
            for y_at in range(n_y):
                for z_at in range(n_z):
                    source = (((x_at + step_x) % n_x) * n_y + (y_at + step_y) % n_y) * n_z + (z_at + step_z) % n_z
                    pairs.append((source, (x_at * n_y + y_at) * n_z + z_at))
        return lax.ppermute(piece, axes, pairs)

    if n_x == 2:
        x_steps = (("pair", 1),)
    else:
        x_steps = (("left", -1), ("right", 1))
    received = {}
    for step_y in (-1, 0, 1):
        for step_z in (-1, 0, 1):
            face = part(part(band, 2, step_y), 3, step_z)
            if step_y or step_z:
                received[(0, step_y, step_z)] = fetch(face, 0, step_y, step_z)
            else:
                received[(0, 0, 0)] = band
            for name, step_x in x_steps:
                if name == "pair":
                    piece = jnp.concatenate([part(face, 1, -1), part(face, 1, 1)], axis=1)
                    got = fetch(piece, step_x, step_y, step_z)
                    received[(-1, step_y, step_z)] = lax.slice_in_dim(got, 0, width, axis=1)
                    received[(1, step_y, step_z)] = lax.slice_in_dim(got, width, 2 * width, axis=1)
                else:
                    received[(step_x, step_y, step_z)] = fetch(part(face, 1, step_x), step_x, step_y, step_z)
    rows_z = []
    for step_z in (-1, 0, 1):
        rows_y = []
        for step_y in (-1, 0, 1):
            rows_y.append(
                jnp.concatenate([received[(step_x, step_y, step_z)] for step_x in (-1, 0, 1)], axis=1)
            )
        rows_z.append(jnp.concatenate(rows_y, axis=2))
    return jnp.concatenate(rows_z, axis=3)


def interpolation_matrix():
    nodes = np.array([-0.8611363116, -0.3399810436, 0.3399810436, 0.8611363116])
    targets = -0.75 + 0.5 * np.arange(4)
    table = np.ones((4, 4))
    for target_row in range(4):
        for node_col in range(4):
            for node_other in range(4):
                if node_other != node_col:
                    table[target_row, node_col] *= (targets[target_row] - nodes[node_other]) / (
                        nodes[node_col] - nodes[node_other]
                    )
    full_table = (
        table[:, None, None, :, None, None]
        * table[None, :, None, None, :, None]
        * table[None, None, :, None, None, :]
    ).reshape(64, 64)
    return jnp.asarray(full_table, dtype=jnp.float32)


def lift_table(length):
    extended = np.eye(length + 8)
    half_count = length // 2 + 4
    even_part = extended[0::2]
    odd_part = extended[1::2]
    odd_one = odd_part[0 : half_count - 1] + LIFT_A * (
        even_part[0 : half_count - 1] + even_part[1:half_count]
    )
    even_two = even_part[1 : half_count - 1] + LIFT_B * (
        odd_one[0 : half_count - 2] + odd_one[1 : half_count - 1]
    )
    odd_three = odd_one[1 : half_count - 2] + LIFT_C * (
        even_two[0 : half_count - 3] + even_two[1 : half_count - 2]
    )
    even_four = even_two[1 : half_count - 3] + LIFT_D * (
        odd_three[0 : half_count - 4] + odd_three[1 : half_count - 3]
    )
    joined = np.concatenate([even_four / LIFT_K, odd_three[1 : length // 2 + 1] * LIFT_K], 0)
    return jnp.asarray(joined, dtype=jnp.float32)


def apply_points(values, matrix):
    return jnp.einsum("qp,fpe->fqe", matrix, values, precision=lax.Precision.HIGHEST)


def to_cells(elements, size_x, size_y, size_z):
    blocks = elements.reshape(3, 4, 4, 4, size_x // 4, size_y // 4, size_z // 4)
    return blocks.transpose(0, 4, 1, 5, 2, 6, 3).reshape(3, size_x, size_y, size_z)


def lift_axis(extended, axis_dim, length):
    table = lift_table(length)
    if axis_dim == 1:
        return jnp.einsum("ab,fbyz->fayz", table, extended, precision=lax.Precision.HIGHEST)
    if axis_dim == 2:
        return jnp.einsum("ab,fxbz->fxaz", table, extended, precision=lax.Precision.HIGHEST)
    return jnp.einsum("fxyb,ab->fxya", extended, table, precision=lax.Precision.HIGHEST)


def spread_table():
    table = np.zeros((32, 4, 128), np.float32)
    for z_index in range(32):
        for c_index in range(4):
            table[z_index, c_index, 4 * z_index + c_index] = 1.0
    return jnp.asarray(table)


def rank_in_owner(target, groups):
    slots_here = target.shape[0]
    block = 128
    blocks = slots_here // block
    owner_ids = jnp.arange(groups, dtype=jnp.int32)
    onehot = (target[None, :] == owner_ids[:, None]).astype(jnp.bfloat16)
    onehot = onehot.reshape(groups, blocks, block)
    upper = (jnp.arange(block)[:, None] < jnp.arange(block)[None, :]).astype(jnp.bfloat16)
    within = jnp.einsum("obk,kj->obj", onehot, upper, preferred_element_type=jnp.float32)
    totals = jnp.sum(onehot.astype(jnp.float32), axis=2)
    block_upper = (jnp.arange(blocks)[:, None] < jnp.arange(blocks)[None, :]).astype(jnp.float32)
    offsets = jnp.dot(totals, block_upper, precision=lax.Precision.HIGHEST)
    counts = within + offsets[:, :, None]
    rank = jnp.sum(onehot.astype(jnp.float32) * counts, axis=0)
    return rank.reshape(slots_here).astype(jnp.int32)


def on_device(point_values, owner, slot, live_count):
    rows_x = lax.axis_size("gx")
    rows_y = lax.axis_size("gy")
    slab_size = rows_x * rows_y
    brick_elems = BX * BY * BZ // 64
    pair_capacity = 2 * brick_elems // slab_size
    slots_here = owner.shape[0]
    width = slab_size * pair_capacity
    flat_values = point_values.reshape(3 * 64, slots_here)
    position = jnp.arange(slots_here, dtype=jnp.int32)
    live = position < live_count[0]
    target = jnp.where(live, owner, slab_size)
    rank = rank_in_owner(target, slab_size)
    column = jnp.where(live, target * pair_capacity + rank, width)
    payload = jnp.concatenate([flat_values, (slot + 1).astype(jnp.float32)[None, :]], axis=0)
    send = jnp.zeros((3 * 64 + 1, width), jnp.float32).at[:, column].set(payload, mode="drop")
    recv = lax.all_to_all(send, ("gx", "gy"), split_axis=1, concat_axis=1, tiled=True)
    marks = recv[3 * 64].astype(jnp.int32)
    recv_slots = jnp.where(marks > 0, marks - 1, brick_elems)
    placed = (
        jnp.zeros((3 * 64, brick_elems), jnp.float32)
        .at[:, recv_slots]
        .set(recv[: 3 * 64], mode="drop")
    )
    matrix = interpolation_matrix()
    elements = jnp.einsum(
        "qp,fpe->fqe", matrix, placed.reshape(3, 64, brick_elems), precision=lax.Precision.HIGHEST
    )
    blocks = elements.reshape(3, 4, 4, 4, BX // 4, BY // 4, BZ // 4)
    coeffs = jnp.einsum(
        "fabcxyz,zcw->fxaybw", blocks, spread_table(), precision=lax.Precision.HIGHEST
    ).reshape(3, BX, BY, BZ)
    for level_index in range(LEVELS):
        size_x = BX >> level_index
        size_y = BY >> level_index
        size_z = BZ >> level_index
        band = coeffs[:, :size_x, :size_y, :size_z]
        widened = halo_pieces(band, 4)
        band = lift_axis(widened, 1, size_x)
        band = lift_axis(band, 2, size_y)
        band = lift_axis(band, 3, size_z)
        coeffs = coeffs.at[:, :size_x, :size_y, :size_z].set(band)
    return coeffs


def solution(mesh):
    in_specs = (
        P(None, None, ("gx", "gy", "gz")),
        P(("gx", "gy", "gz")),
        P(("gx", "gy", "gz")),
        P(("gx", "gy", "gz")),
    )
    out_specs = P(None, "gx", "gy", "gz")
    return jax.shard_map(
        on_device, mesh=mesh, in_specs=in_specs, out_specs=out_specs, check_vma=False
    )
```

```python
import jax
import jax.numpy as jnp
import numpy as np
from jax import lax
from jax.sharding import PartitionSpec as P

BX = 32
BY = 32
BZ = 128
LEVELS = 3


LIFT_A = -1.586134342
LIFT_B = -0.05298011854
LIFT_C = 0.8829110762
LIFT_D = 0.4435068522
LIFT_K = 1.149604398


def shift_pairs(count, step):
    return [(i, (i + step) % count) for i in range(count)]


def extended_2(cells, sides, width):
    for axis, dim in sides:
        count = lax.axis_size(axis)
        size = cells.shape[dim]
        head = lax.slice_in_dim(cells, 0, width, axis=dim)
        tail = lax.slice_in_dim(cells, size - width, size, axis=dim)
        if count == 2:
            both = lax.ppermute(jnp.concatenate([tail, head], axis=dim), axis, shift_pairs(count, 1))
            left = lax.slice_in_dim(both, 0, width, axis=dim)
            right = lax.slice_in_dim(both, width, 2 * width, axis=dim)
        elif dim == cells.ndim - 1:
            def packed(piece):
                moved = jnp.moveaxis(piece, dim, 1)
                return moved.reshape(moved.shape[:2] + (-1,))

            def unpacked(flat):
                moved = flat.reshape((flat.shape[0], width) + cells.shape[1:dim])
                return jnp.moveaxis(moved, 1, dim)

            left = unpacked(lax.ppermute(packed(tail), axis, shift_pairs(count, 1)))
            right = unpacked(lax.ppermute(packed(head), axis, shift_pairs(count, -1)))
        else:
            left = lax.ppermute(tail, axis, shift_pairs(count, 1))
            right = lax.ppermute(head, axis, shift_pairs(count, -1))
        cells = jnp.concatenate([left, cells, right], axis=dim)
    return cells


def interpolation_matrix():
    nodes = np.array([-0.8611363116, -0.3399810436, 0.3399810436, 0.8611363116])
    targets = -0.75 + 0.5 * np.arange(4)
    table = np.ones((4, 4))
    for target_row in range(4):
        for node_col in range(4):
            for node_other in range(4):
                if node_other != node_col:
                    table[target_row, node_col] *= (targets[target_row] - nodes[node_other]) / (
                        nodes[node_col] - nodes[node_other]
                    )
    full_table = (
        table[:, None, None, :, None, None]
        * table[None, :, None, None, :, None]
        * table[None, None, :, None, None, :]
    ).reshape(64, 64)
    return jnp.asarray(full_table, dtype=jnp.float32)


def lift_table(length):
    extended = np.eye(length + 8)
    half_count = length // 2 + 4
    even_part = extended[0::2]
    odd_part = extended[1::2]
    odd_one = odd_part[0 : half_count - 1] + LIFT_A * (
        even_part[0 : half_count - 1] + even_part[1:half_count]
    )
    even_two = even_part[1 : half_count - 1] + LIFT_B * (
        odd_one[0 : half_count - 2] + odd_one[1 : half_count - 1]
    )
    odd_three = odd_one[1 : half_count - 2] + LIFT_C * (
        even_two[0 : half_count - 3] + even_two[1 : half_count - 2]
    )
    even_four = even_two[1 : half_count - 3] + LIFT_D * (
        odd_three[0 : half_count - 4] + odd_three[1 : half_count - 3]
    )
    joined = np.concatenate([even_four / LIFT_K, odd_three[1 : length // 2 + 1] * LIFT_K], 0)
    return jnp.asarray(joined, dtype=jnp.float32)


def apply_points(values, matrix):
    return jnp.einsum("qp,fpe->fqe", matrix, values, precision=lax.Precision.HIGHEST)


def to_cells(elements, size_x, size_y, size_z):
    blocks = elements.reshape(3, 4, 4, 4, size_x // 4, size_y // 4, size_z // 4)
    return blocks.transpose(0, 4, 1, 5, 2, 6, 3).reshape(3, size_x, size_y, size_z)


def lift_axis(extended, axis_dim, length):
    table = lift_table(length)
    if axis_dim == 1:
        return jnp.einsum("ab,fbyz->fayz", table, extended, precision=lax.Precision.HIGHEST)
    if axis_dim == 2:
        return jnp.einsum("ab,fxbz->fxaz", table, extended, precision=lax.Precision.HIGHEST)
    return jnp.einsum("fxyb,ab->fxya", extended, table, precision=lax.Precision.HIGHEST)


def spread_table():
    table = np.zeros((32, 4, 128), np.float32)
    for z_index in range(32):
        for c_index in range(4):
            table[z_index, c_index, 4 * z_index + c_index] = 1.0
    return jnp.asarray(table)


def rank_in_owner(target, groups):
    slots_here = target.shape[0]
    block = 128
    blocks = slots_here // block
    owner_ids = jnp.arange(groups, dtype=jnp.int32)
    onehot = (target[None, :] == owner_ids[:, None]).astype(jnp.bfloat16)
    onehot = onehot.reshape(groups, blocks, block)
    upper = (jnp.arange(block)[:, None] < jnp.arange(block)[None, :]).astype(jnp.bfloat16)
    within = jnp.einsum("obk,kj->obj", onehot, upper, preferred_element_type=jnp.float32)
    totals = jnp.sum(onehot.astype(jnp.float32), axis=2)
    block_upper = (jnp.arange(blocks)[:, None] < jnp.arange(blocks)[None, :]).astype(jnp.float32)
    offsets = jnp.dot(totals, block_upper, precision=lax.Precision.HIGHEST)
    counts = within + offsets[:, :, None]
    rank = jnp.sum(onehot.astype(jnp.float32) * counts, axis=0)
    return rank.reshape(slots_here).astype(jnp.int32)


def on_device(point_values, owner, slot, live_count):
    rows_x = lax.axis_size("gx")
    rows_y = lax.axis_size("gy")
    slab_size = rows_x * rows_y
    brick_elems = BX * BY * BZ // 64
    pair_capacity = 2 * brick_elems // slab_size
    slots_here = owner.shape[0]
    width = slab_size * pair_capacity
    flat_values = point_values.reshape(3 * 64, slots_here)
    position = jnp.arange(slots_here, dtype=jnp.int32)
    live = position < live_count[0]
    target = jnp.where(live, owner, slab_size)
    rank = rank_in_owner(target, slab_size)
    column = jnp.where(live, target * pair_capacity + rank, width)
    payload = jnp.concatenate([flat_values, (slot + 1).astype(jnp.float32)[None, :]], axis=0)
    send = jnp.zeros((3 * 64 + 1, width), jnp.float32).at[:, column].set(payload, mode="drop")
    recv = lax.all_to_all(send, ("gx", "gy"), split_axis=1, concat_axis=1, tiled=True)
    marks = recv[3 * 64].astype(jnp.int32)
    recv_slots = jnp.where(marks > 0, marks - 1, brick_elems)
    placed = (
        jnp.zeros((3 * 64, brick_elems), jnp.float32)
        .at[:, recv_slots]
        .set(recv[: 3 * 64], mode="drop")
    )
    matrix = interpolation_matrix()
    elements = jnp.einsum(
        "qp,fpe->fqe", matrix, placed.reshape(3, 64, brick_elems), precision=lax.Precision.HIGHEST
    )
    blocks = elements.reshape(3, 4, 4, 4, BX // 4, BY // 4, BZ // 4)
    coeffs = jnp.einsum(
        "fabcxyz,zcw->fxaybw", blocks, spread_table(), precision=lax.Precision.HIGHEST
    ).reshape(3, BX, BY, BZ)
    for level_index in range(LEVELS):
        size_x = BX >> level_index
        size_y = BY >> level_index
        size_z = BZ >> level_index
        band = coeffs[:, :size_x, :size_y, :size_z]
        widened = extended_2(band, (("gx", 1),), 4)
        band = lift_axis(widened, 1, size_x)
        widened = extended_2(band, (("gy", 2),), 4)
        band = lift_axis(widened, 2, size_y)
        widened = extended_2(band, (("gz", 3),), 4)
        band = lift_axis(widened, 3, size_z)
        coeffs = coeffs.at[:, :size_x, :size_y, :size_z].set(band)
    return coeffs


def solution(mesh):
    in_specs = (
        P(None, None, ("gx", "gy", "gz")),
        P(("gx", "gy", "gz")),
        P(("gx", "gy", "gz")),
        P(("gx", "gy", "gz")),
    )
    out_specs = P(None, "gx", "gy", "gz")
    return jax.shard_map(
        on_device, mesh=mesh, in_specs=in_specs, out_specs=out_specs, check_vma=False
    )
```

```python
import jax
import jax.numpy as jnp
import numpy as np
from jax import lax
from jax.sharding import PartitionSpec as P

BX = 32
BY = 32
BZ = 128
LEVELS = 3


LIFT_A = -1.586134342
LIFT_B = -0.05298011854
LIFT_C = 0.8829110762
LIFT_D = 0.4435068522
LIFT_K = 1.149604398


def shift_pairs(count, step):
    return [(i, (i + step) % count) for i in range(count)]


def extended_2(cells, sides, width):
    for axis, dim in sides:
        count = lax.axis_size(axis)
        size = cells.shape[dim]
        head = lax.slice_in_dim(cells, 0, width, axis=dim)
        tail = lax.slice_in_dim(cells, size - width, size, axis=dim)
        if count == 2:
            both = lax.ppermute(jnp.concatenate([tail, head], axis=dim), axis, shift_pairs(count, 1))
            left = lax.slice_in_dim(both, 0, width, axis=dim)
            right = lax.slice_in_dim(both, width, 2 * width, axis=dim)
        elif dim == cells.ndim - 1:
            def packed(piece):
                moved = jnp.moveaxis(piece, dim, 1)
                return moved.reshape(moved.shape[:2] + (-1,))

            def unpacked(flat):
                moved = flat.reshape((flat.shape[0], width) + cells.shape[1:dim])
                return jnp.moveaxis(moved, 1, dim)

            left = unpacked(lax.ppermute(packed(tail), axis, shift_pairs(count, 1)))
            right = unpacked(lax.ppermute(packed(head), axis, shift_pairs(count, -1)))
        else:
            left = lax.ppermute(tail, axis, shift_pairs(count, 1))
            right = lax.ppermute(head, axis, shift_pairs(count, -1))
        cells = jnp.concatenate([left, cells, right], axis=dim)
    return cells


def interpolation_matrix():
    nodes = np.array([-0.8611363116, -0.3399810436, 0.3399810436, 0.8611363116])
    targets = -0.75 + 0.5 * np.arange(4)
    table = np.ones((4, 4))
    for target_row in range(4):
        for node_col in range(4):
            for node_other in range(4):
                if node_other != node_col:
                    table[target_row, node_col] *= (targets[target_row] - nodes[node_other]) / (
                        nodes[node_col] - nodes[node_other]
                    )
    full_table = (
        table[:, None, None, :, None, None]
        * table[None, :, None, None, :, None]
        * table[None, None, :, None, None, :]
    ).reshape(64, 64)
    return jnp.asarray(full_table, dtype=jnp.float32)


def lift_table(length):
    extended = np.eye(length + 8)
    half_count = length // 2 + 4
    even_part = extended[0::2]
    odd_part = extended[1::2]
    odd_one = odd_part[0 : half_count - 1] + LIFT_A * (
        even_part[0 : half_count - 1] + even_part[1:half_count]
    )
    even_two = even_part[1 : half_count - 1] + LIFT_B * (
        odd_one[0 : half_count - 2] + odd_one[1 : half_count - 1]
    )
    odd_three = odd_one[1 : half_count - 2] + LIFT_C * (
        even_two[0 : half_count - 3] + even_two[1 : half_count - 2]
    )
    even_four = even_two[1 : half_count - 3] + LIFT_D * (
        odd_three[0 : half_count - 4] + odd_three[1 : half_count - 3]
    )
    joined = np.concatenate([even_four / LIFT_K, odd_three[1 : length // 2 + 1] * LIFT_K], 0)
    return jnp.asarray(joined, dtype=jnp.float32)


def apply_points(values, matrix):
    return jnp.einsum("qp,fpe->fqe", matrix, values, precision=lax.Precision.HIGHEST)


def to_cells(elements, size_x, size_y, size_z):
    blocks = elements.reshape(3, 4, 4, 4, size_x // 4, size_y // 4, size_z // 4)
    return blocks.transpose(0, 4, 1, 5, 2, 6, 3).reshape(3, size_x, size_y, size_z)


def lift_axis(extended, axis_dim, length):
    table = lift_table(length)
    if axis_dim == 1:
        return jnp.einsum("ab,fbyz->fayz", table, extended, precision=lax.Precision.HIGHEST)
    if axis_dim == 2:
        return jnp.einsum("ab,fxbz->fxaz", table, extended, precision=lax.Precision.HIGHEST)
    return jnp.einsum("fxyb,ab->fxya", extended, table, precision=lax.Precision.HIGHEST)


def spread_table():
    table = np.zeros((32, 4, 128), np.float32)
    for z_index in range(32):
        for c_index in range(4):
            table[z_index, c_index, 4 * z_index + c_index] = 1.0
    return jnp.asarray(table)


def rank_in_owner(target, groups):
    slots_here = target.shape[0]
    block = 128
    blocks = slots_here // block
    owner_ids = jnp.arange(groups, dtype=jnp.int32)
    onehot = (target[None, :] == owner_ids[:, None]).astype(jnp.bfloat16)
    onehot = onehot.reshape(groups, blocks, block)
    upper = (jnp.arange(block)[:, None] < jnp.arange(block)[None, :]).astype(jnp.bfloat16)
    within = jnp.einsum("obk,kj->obj", onehot, upper, preferred_element_type=jnp.float32)
    totals = jnp.sum(onehot.astype(jnp.float32), axis=2)
    block_upper = (jnp.arange(blocks)[:, None] < jnp.arange(blocks)[None, :]).astype(jnp.float32)
    offsets = jnp.dot(totals, block_upper, precision=lax.Precision.HIGHEST)
    counts = within + offsets[:, :, None]
    rank = jnp.sum(onehot.astype(jnp.float32) * counts, axis=0)
    return rank.reshape(slots_here).astype(jnp.int32)


def on_device(point_values, owner, slot, live_count):
    rows_x = lax.axis_size("gx")
    rows_y = lax.axis_size("gy")
    slab_size = rows_x * rows_y
    brick_elems = BX * BY * BZ // 64
    pair_capacity = 2 * brick_elems // slab_size
    slots_here = owner.shape[0]
    width = slab_size * pair_capacity
    flat_values = point_values.reshape(3 * 64, slots_here)
    position = jnp.arange(slots_here, dtype=jnp.int32)
    live = position < live_count[0]
    target = jnp.where(live, owner, slab_size)
    rank = rank_in_owner(target, slab_size)
    column = jnp.where(live, target * pair_capacity + rank, width)
    payload = jnp.concatenate([flat_values, (slot + 1).astype(jnp.float32)[None, :]], axis=0)
    send = jnp.zeros((3 * 64 + 1, width), jnp.float32).at[:, column].set(payload, mode="drop")
    recv = lax.all_to_all(send, ("gx", "gy"), split_axis=1, concat_axis=1, tiled=True)
    marks = recv[3 * 64].astype(jnp.int32)
    recv_slots = jnp.where(marks > 0, marks - 1, brick_elems)
    placed = (
        jnp.zeros((3 * 64, brick_elems), jnp.float32)
        .at[:, recv_slots]
        .set(recv[: 3 * 64], mode="drop")
    )
    matrix = interpolation_matrix()
    elements = jnp.einsum(
        "qp,fpe->fqe", matrix, placed.reshape(3, 64, brick_elems), precision=lax.Precision.HIGHEST
    )
    blocks = elements.reshape(3, 4, 4, 4, BX // 4, BY // 4, BZ // 4)
    coeffs = jnp.einsum(
        "fabcxyz,zcw->fxaybw", blocks, spread_table(), precision=lax.Precision.HIGHEST
    ).reshape(3, BX, BY, BZ)
    bands = []
    band = coeffs
    for level_index in range(LEVELS):
        size_x = BX >> level_index
        size_y = BY >> level_index
        size_z = BZ >> level_index
        band = band[:, :size_x, :size_y, :size_z]
        widened = extended_2(band, (("gx", 1),), 4)
        band = lift_axis(widened, 1, size_x)
        widened = extended_2(band, (("gy", 2),), 4)
        band = lift_axis(widened, 2, size_y)
        widened = extended_2(band, (("gz", 3),), 4)
        band = lift_axis(widened, 3, size_z)
        bands.append(band)
    result = bands[-1]
    for outer in reversed(bands[:-1]):
        padding = [(0, 0)] + [(0, outer.shape[d] - result.shape[d]) for d in range(1, 4)]
        inside = (
            (lax.broadcasted_iota(jnp.int32, outer.shape, 1) < result.shape[1])
            & (lax.broadcasted_iota(jnp.int32, outer.shape, 2) < result.shape[2])
            & (lax.broadcasted_iota(jnp.int32, outer.shape, 3) < result.shape[3])
        )
        result = jnp.where(inside, jnp.pad(result, padding), outer)
    return result


def solution(mesh):
    in_specs = (
        P(None, None, ("gx", "gy", "gz")),
        P(("gx", "gy", "gz")),
        P(("gx", "gy", "gz")),
        P(("gx", "gy", "gz")),
    )
    out_specs = P(None, "gx", "gy", "gz")
    return jax.shard_map(
        on_device, mesh=mesh, in_specs=in_specs, out_specs=out_specs, check_vma=False
    )
```

```python
import jax
import jax.numpy as jnp
import numpy as np
from jax import lax
from jax.sharding import PartitionSpec as P

BX = 32
BY = 32
BZ = 128
LEVELS = 3


LIFT_A = -1.586134342
LIFT_B = -0.05298011854
LIFT_C = 0.8829110762
LIFT_D = 0.4435068522
LIFT_K = 1.149604398


def shift_pairs(count, step):
    return [(i, (i + step) % count) for i in range(count)]


def halo_sides(cells, axis, dim, width):
    count = lax.axis_size(axis)
    size = cells.shape[dim]
    head = lax.slice_in_dim(cells, 0, width, axis=dim)
    tail = lax.slice_in_dim(cells, size - width, size, axis=dim)
    if count == 2:
        both = lax.ppermute(jnp.concatenate([tail, head], axis=dim), axis, shift_pairs(count, 1))
        return lax.slice_in_dim(both, 0, width, axis=dim), lax.slice_in_dim(both, width, 2 * width, axis=dim)
    if dim == cells.ndim - 1:
        def packed(piece):
            moved = jnp.moveaxis(piece, dim, 1)
            return moved.reshape(moved.shape[:2] + (-1,))

        def unpacked(flat):
            moved = flat.reshape((flat.shape[0], width) + cells.shape[1:dim])
            return jnp.moveaxis(moved, 1, dim)

        left = unpacked(lax.ppermute(packed(tail), axis, shift_pairs(count, 1)))
        right = unpacked(lax.ppermute(packed(head), axis, shift_pairs(count, -1)))
        return left, right
    left = lax.ppermute(tail, axis, shift_pairs(count, 1))
    right = lax.ppermute(head, axis, shift_pairs(count, -1))
    return left, right


def interpolation_matrix():
    nodes = np.array([-0.8611363116, -0.3399810436, 0.3399810436, 0.8611363116])
    targets = -0.75 + 0.5 * np.arange(4)
    table = np.ones((4, 4))
    for target_row in range(4):
        for node_col in range(4):
            for node_other in range(4):
                if node_other != node_col:
                    table[target_row, node_col] *= (targets[target_row] - nodes[node_other]) / (
                        nodes[node_col] - nodes[node_other]
                    )
    full_table = (
        table[:, None, None, :, None, None]
        * table[None, :, None, None, :, None]
        * table[None, None, :, None, None, :]
    ).reshape(64, 64)
    return jnp.asarray(full_table, dtype=jnp.float32)


def lift_table(length):
    extended = np.eye(length + 8)
    half_count = length // 2 + 4
    even_part = extended[0::2]
    odd_part = extended[1::2]
    odd_one = odd_part[0 : half_count - 1] + LIFT_A * (
        even_part[0 : half_count - 1] + even_part[1:half_count]
    )
    even_two = even_part[1 : half_count - 1] + LIFT_B * (
        odd_one[0 : half_count - 2] + odd_one[1 : half_count - 1]
    )
    odd_three = odd_one[1 : half_count - 2] + LIFT_C * (
        even_two[0 : half_count - 3] + even_two[1 : half_count - 2]
    )
    even_four = even_two[1 : half_count - 3] + LIFT_D * (
        odd_three[0 : half_count - 4] + odd_three[1 : half_count - 3]
    )
    joined = np.concatenate([even_four / LIFT_K, odd_three[1 : length // 2 + 1] * LIFT_K], 0)
    return jnp.asarray(joined, dtype=jnp.float32)


def apply_points(values, matrix):
    return jnp.einsum("qp,fpe->fqe", matrix, values, precision=lax.Precision.HIGHEST)


def to_cells(elements, size_x, size_y, size_z):
    blocks = elements.reshape(3, 4, 4, 4, size_x // 4, size_y // 4, size_z // 4)
    return blocks.transpose(0, 4, 1, 5, 2, 6, 3).reshape(3, size_x, size_y, size_z)


def apply_table(table, cells, axis_dim):
    if axis_dim == 1:
        return jnp.einsum("ab,fbyz->fayz", table, cells, precision=lax.Precision.HIGHEST)
    if axis_dim == 2:
        return jnp.einsum("ab,fxbz->fxaz", table, cells, precision=lax.Precision.HIGHEST)
    return jnp.einsum("fxyb,ab->fxya", cells, table, precision=lax.Precision.HIGHEST)


def lift_axis(cells, axis, axis_dim, width):
    length = cells.shape[axis_dim]
    left, right = halo_sides(cells, axis, axis_dim, width)
    table = lift_table(length)
    inner = apply_table(table[:, width : width + length], cells, axis_dim)
    edges = apply_table(table[:, :width], left, axis_dim) + apply_table(
        table[:, width + length :], right, axis_dim
    )
    return inner + edges


def spread_table():
    table = np.zeros((32, 4, 128), np.float32)
    for z_index in range(32):
        for c_index in range(4):
            table[z_index, c_index, 4 * z_index + c_index] = 1.0
    return jnp.asarray(table)


def rank_in_owner(target, groups):
    slots_here = target.shape[0]
    block = 128
    blocks = slots_here // block
    owner_ids = jnp.arange(groups, dtype=jnp.int32)
    onehot = (target[None, :] == owner_ids[:, None]).astype(jnp.bfloat16)
    onehot = onehot.reshape(groups, blocks, block)
    upper = (jnp.arange(block)[:, None] < jnp.arange(block)[None, :]).astype(jnp.bfloat16)
    within = jnp.einsum("obk,kj->obj", onehot, upper, preferred_element_type=jnp.float32)
    totals = jnp.sum(onehot.astype(jnp.float32), axis=2)
    block_upper = (jnp.arange(blocks)[:, None] < jnp.arange(blocks)[None, :]).astype(jnp.float32)
    offsets = jnp.dot(totals, block_upper, precision=lax.Precision.HIGHEST)
    counts = within + offsets[:, :, None]
    rank = jnp.sum(onehot.astype(jnp.float32) * counts, axis=0)
    return rank.reshape(slots_here).astype(jnp.int32)


def on_device(point_values, owner, slot, live_count):
    rows_x = lax.axis_size("gx")
    rows_y = lax.axis_size("gy")
    slab_size = rows_x * rows_y
    brick_elems = BX * BY * BZ // 64
    pair_capacity = 2 * brick_elems // slab_size
    slots_here = owner.shape[0]
    width = slab_size * pair_capacity
    flat_values = point_values.reshape(3 * 64, slots_here)
    position = jnp.arange(slots_here, dtype=jnp.int32)
    live = position < live_count[0]
    target = jnp.where(live, owner, slab_size)
    rank = rank_in_owner(target, slab_size)
    column = jnp.where(live, target * pair_capacity + rank, width)
    payload = jnp.concatenate([flat_values, (slot + 1).astype(jnp.float32)[None, :]], axis=0)
    send = jnp.zeros((3 * 64 + 1, width), jnp.float32).at[:, column].set(payload, mode="drop")
    recv = lax.all_to_all(send, ("gx", "gy"), split_axis=1, concat_axis=1, tiled=True)
    marks = recv[3 * 64].astype(jnp.int32)
    recv_slots = jnp.where(marks > 0, marks - 1, brick_elems)
    placed = (
        jnp.zeros((3 * 64, brick_elems), jnp.float32)
        .at[:, recv_slots]
        .set(recv[: 3 * 64], mode="drop")
    )
    matrix = interpolation_matrix()
    elements = jnp.einsum(
        "qp,fpe->fqe", matrix, placed.reshape(3, 64, brick_elems), precision=lax.Precision.HIGHEST
    )
    blocks = elements.reshape(3, 4, 4, 4, BX // 4, BY // 4, BZ // 4)
    coeffs = jnp.einsum(
        "fabcxyz,zcw->fxaybw", blocks, spread_table(), precision=lax.Precision.HIGHEST
    ).reshape(3, BX, BY, BZ)
    bands = []
    band = coeffs
    for level_index in range(LEVELS):
        size_x = BX >> level_index
        size_y = BY >> level_index
        size_z = BZ >> level_index
        band = band[:, :size_x, :size_y, :size_z]
        band = lift_axis(band, "gx", 1, 4)
        band = lift_axis(band, "gy", 2, 4)
        band = lift_axis(band, "gz", 3, 4)
        bands.append(band)
    result = bands[-1]
    for outer in reversed(bands[:-1]):
        padding = [(0, 0)] + [(0, outer.shape[d] - result.shape[d]) for d in range(1, 4)]
        inside = (
            (lax.broadcasted_iota(jnp.int32, outer.shape, 1) < result.shape[1])
            & (lax.broadcasted_iota(jnp.int32, outer.shape, 2) < result.shape[2])
            & (lax.broadcasted_iota(jnp.int32, outer.shape, 3) < result.shape[3])
        )
        result = jnp.where(inside, jnp.pad(result, padding), outer)
    return result


def solution(mesh):
    in_specs = (
        P(None, None, ("gx", "gy", "gz")),
        P(("gx", "gy", "gz")),
        P(("gx", "gy", "gz")),
        P(("gx", "gy", "gz")),
    )
    out_specs = P(None, "gx", "gy", "gz")
    return jax.shard_map(
        on_device, mesh=mesh, in_specs=in_specs, out_specs=out_specs, check_vma=False
    )
```

```python
import jax
import jax.numpy as jnp
import numpy as np
from jax import lax
from jax.sharding import PartitionSpec as P

BX = 32
BY = 32
BZ = 128
LEVELS = 3


LIFT_A = -1.586134342
LIFT_B = -0.05298011854
LIFT_C = 0.8829110762
LIFT_D = 0.4435068522
LIFT_K = 1.149604398


def shift_pairs(count, step):
    return [(i, (i + step) % count) for i in range(count)]


def extended_2(cells, sides, width):
    for axis, dim in sides:
        count = lax.axis_size(axis)
        size = cells.shape[dim]
        head = lax.slice_in_dim(cells, 0, width, axis=dim)
        tail = lax.slice_in_dim(cells, size - width, size, axis=dim)
        if count == 2:
            both = lax.ppermute(jnp.concatenate([tail, head], axis=dim), axis, shift_pairs(count, 1))
            left = lax.slice_in_dim(both, 0, width, axis=dim)
            right = lax.slice_in_dim(both, width, 2 * width, axis=dim)
        elif dim == cells.ndim - 1:
            def packed(piece):
                moved = jnp.moveaxis(piece, dim, 1)
                return moved.reshape(moved.shape[:2] + (-1,))

            def unpacked(flat):
                moved = flat.reshape((flat.shape[0], width) + cells.shape[1:dim])
                return jnp.moveaxis(moved, 1, dim)

            left = unpacked(lax.ppermute(packed(tail), axis, shift_pairs(count, 1)))
            right = unpacked(lax.ppermute(packed(head), axis, shift_pairs(count, -1)))
        else:
            left = lax.ppermute(tail, axis, shift_pairs(count, 1))
            right = lax.ppermute(head, axis, shift_pairs(count, -1))
        cells = jnp.concatenate([left, cells, right], axis=dim)
    return cells


def interpolation_matrix():
    nodes = np.array([-0.8611363116, -0.3399810436, 0.3399810436, 0.8611363116])
    targets = -0.75 + 0.5 * np.arange(4)
    table = np.ones((4, 4))
    for target_row in range(4):
        for node_col in range(4):
            for node_other in range(4):
                if node_other != node_col:
                    table[target_row, node_col] *= (targets[target_row] - nodes[node_other]) / (
                        nodes[node_col] - nodes[node_other]
                    )
    full_table = (
        table[:, None, None, :, None, None]
        * table[None, :, None, None, :, None]
        * table[None, None, :, None, None, :]
    ).reshape(64, 64)
    return jnp.asarray(full_table, dtype=jnp.float32)


def lift_table(length):
    extended = np.eye(length + 8)
    half_count = length // 2 + 4
    even_part = extended[0::2]
    odd_part = extended[1::2]
    odd_one = odd_part[0 : half_count - 1] + LIFT_A * (
        even_part[0 : half_count - 1] + even_part[1:half_count]
    )
    even_two = even_part[1 : half_count - 1] + LIFT_B * (
        odd_one[0 : half_count - 2] + odd_one[1 : half_count - 1]
    )
    odd_three = odd_one[1 : half_count - 2] + LIFT_C * (
        even_two[0 : half_count - 3] + even_two[1 : half_count - 2]
    )
    even_four = even_two[1 : half_count - 3] + LIFT_D * (
        odd_three[0 : half_count - 4] + odd_three[1 : half_count - 3]
    )
    joined = np.concatenate([even_four / LIFT_K, odd_three[1 : length // 2 + 1] * LIFT_K], 0)
    return jnp.asarray(joined, dtype=jnp.float32)


def wide_table(length, halo, low_extra):
    extended = np.eye(length + 2 * halo)
    half_count = length // 2 + halo
    even_part = extended[0::2]
    odd_part = extended[1::2]
    odd_one = odd_part[0 : half_count - 1] + LIFT_A * (
        even_part[0 : half_count - 1] + even_part[1:half_count]
    )
    even_two = even_part[1 : half_count - 1] + LIFT_B * (
        odd_one[0 : half_count - 2] + odd_one[1 : half_count - 1]
    )
    odd_three = odd_one[1 : half_count - 2] + LIFT_C * (
        even_two[0 : half_count - 3] + even_two[1 : half_count - 2]
    )
    even_four = even_two[1 : half_count - 3] + LIFT_D * (
        odd_three[0 : half_count - 4] + odd_three[1 : half_count - 3]
    )
    low_at = halo // 2 - 2 - low_extra
    high_at = halo // 2 - 1
    joined = np.concatenate(
        [
            even_four[low_at : low_at + length // 2 + 2 * low_extra] / LIFT_K,
            odd_three[high_at : high_at + length // 2] * LIFT_K,
        ],
        0,
    )
    return jnp.asarray(joined, dtype=jnp.float32)


def apply_table(table, cells, axis_dim):
    if axis_dim == 1:
        return jnp.einsum("ab,fbyz->fayz", table, cells, precision=lax.Precision.HIGHEST)
    if axis_dim == 2:
        return jnp.einsum("ab,fxbz->fxaz", table, cells, precision=lax.Precision.HIGHEST)
    return jnp.einsum("fxyb,ab->fxya", cells, table, precision=lax.Precision.HIGHEST)


def apply_points(values, matrix):
    return jnp.einsum("qp,fpe->fqe", matrix, values, precision=lax.Precision.HIGHEST)


def to_cells(elements, size_x, size_y, size_z):
    blocks = elements.reshape(3, 4, 4, 4, size_x // 4, size_y // 4, size_z // 4)
    return blocks.transpose(0, 4, 1, 5, 2, 6, 3).reshape(3, size_x, size_y, size_z)


def lift_axis(extended, axis_dim, length):
    table = lift_table(length)
    if axis_dim == 1:
        return jnp.einsum("ab,fbyz->fayz", table, extended, precision=lax.Precision.HIGHEST)
    if axis_dim == 2:
        return jnp.einsum("ab,fxbz->fxaz", table, extended, precision=lax.Precision.HIGHEST)
    return jnp.einsum("fxyb,ab->fxya", extended, table, precision=lax.Precision.HIGHEST)


def spread_table():
    table = np.zeros((32, 4, 128), np.float32)
    for z_index in range(32):
        for c_index in range(4):
            table[z_index, c_index, 4 * z_index + c_index] = 1.0
    return jnp.asarray(table)


def rank_in_owner(target, groups):
    slots_here = target.shape[0]
    block = 128
    blocks = slots_here // block
    owner_ids = jnp.arange(groups, dtype=jnp.int32)
    onehot = (target[None, :] == owner_ids[:, None]).astype(jnp.bfloat16)
    onehot = onehot.reshape(groups, blocks, block)
    upper = (jnp.arange(block)[:, None] < jnp.arange(block)[None, :]).astype(jnp.bfloat16)
    within = jnp.einsum("obk,kj->obj", onehot, upper, preferred_element_type=jnp.float32)
    totals = jnp.sum(onehot.astype(jnp.float32), axis=2)
    block_upper = (jnp.arange(blocks)[:, None] < jnp.arange(blocks)[None, :]).astype(jnp.float32)
    offsets = jnp.dot(totals, block_upper, precision=lax.Precision.HIGHEST)
    counts = within + offsets[:, :, None]
    rank = jnp.sum(onehot.astype(jnp.float32) * counts, axis=0)
    return rank.reshape(slots_here).astype(jnp.int32)


def on_device(point_values, owner, slot, live_count):
    rows_x = lax.axis_size("gx")
    rows_y = lax.axis_size("gy")
    slab_size = rows_x * rows_y
    brick_elems = BX * BY * BZ // 64
    pair_capacity = 2 * brick_elems // slab_size
    slots_here = owner.shape[0]
    width = slab_size * pair_capacity
    flat_values = point_values.reshape(3 * 64, slots_here)
    position = jnp.arange(slots_here, dtype=jnp.int32)
    live = position < live_count[0]
    target = jnp.where(live, owner, slab_size)
    rank = rank_in_owner(target, slab_size)
    column = jnp.where(live, target * pair_capacity + rank, width)
    payload = jnp.concatenate([flat_values, (slot + 1).astype(jnp.float32)[None, :]], axis=0)
    send = jnp.zeros((3 * 64 + 1, width), jnp.float32).at[:, column].set(payload, mode="drop")
    recv = lax.all_to_all(send, ("gx", "gy"), split_axis=1, concat_axis=1, tiled=True)
    marks = recv[3 * 64].astype(jnp.int32)
    recv_slots = jnp.where(marks > 0, marks - 1, brick_elems)
    placed = (
        jnp.zeros((3 * 64, brick_elems), jnp.float32)
        .at[:, recv_slots]
        .set(recv[: 3 * 64], mode="drop")
    )
    matrix = interpolation_matrix()
    elements = jnp.einsum(
        "qp,fpe->fqe", matrix, placed.reshape(3, 64, brick_elems), precision=lax.Precision.HIGHEST
    )
    blocks = elements.reshape(3, 4, 4, 4, BX // 4, BY // 4, BZ // 4)
    coeffs = jnp.einsum(
        "fabcxyz,zcw->fxaybw", blocks, spread_table(), precision=lax.Precision.HIGHEST
    ).reshape(3, BX, BY, BZ)
    band = coeffs
    widened = extended_2(band, (("gx", 1),), 4)
    band = lift_axis(widened, 1, BX)
    widened = extended_2(band, (("gy", 2),), 4)
    band = lift_axis(widened, 2, BY)
    widened = extended_2(band, (("gz", 3),), 4)
    first = lift_axis(widened, 3, BZ)
    deep = 12
    reach = 4
    sizes = (BX // 2, BY // 2, BZ // 2)
    band = first[:, : sizes[0], : sizes[1], : sizes[2]]
    widened = extended_2(band, (("gx", 1), ("gy", 2), ("gz", 3)), deep)
    for dim, size in zip((1, 2, 3), sizes):
        widened = apply_table(wide_table(size, deep, reach), widened, dim)
    second = widened
    for dim, size in zip((1, 2, 3), sizes):
        low_local = lax.slice_in_dim(second, reach, reach + size // 2, axis=dim)
        high_local = lax.slice_in_dim(second, size // 2 + 2 * reach, size + 2 * reach, axis=dim)
        second = jnp.concatenate([low_local, high_local], axis=dim)
    inner = widened[:, : sizes[0] // 2 + 2 * reach, : sizes[1] // 2 + 2 * reach, : sizes[2] // 2 + 2 * reach]
    third = lift_axis(inner, 1, sizes[0] // 2)
    third = lift_axis(third, 2, sizes[1] // 2)
    third = lift_axis(third, 3, sizes[2] // 2)
    result = third
    for outer in (second, first):
        padding = [(0, 0)] + [(0, outer.shape[d] - result.shape[d]) for d in range(1, 4)]
        inside = (
            (lax.broadcasted_iota(jnp.int32, outer.shape, 1) < result.shape[1])
            & (lax.broadcasted_iota(jnp.int32, outer.shape, 2) < result.shape[2])
            & (lax.broadcasted_iota(jnp.int32, outer.shape, 3) < result.shape[3])
        )
        result = jnp.where(inside, jnp.pad(result, padding), outer)
    return result


def solution(mesh):
    in_specs = (
        P(None, None, ("gx", "gy", "gz")),
        P(("gx", "gy", "gz")),
        P(("gx", "gy", "gz")),
        P(("gx", "gy", "gz")),
    )
    out_specs = P(None, "gx", "gy", "gz")
    return jax.shard_map(
        on_device, mesh=mesh, in_specs=in_specs, out_specs=out_specs, check_vma=False
    )
```

```python
import jax
import jax.numpy as jnp
import numpy as np
from jax import lax
from jax.sharding import PartitionSpec as P

BX = 32
BY = 32
BZ = 128
LEVELS = 3


LIFT_A = -1.586134342
LIFT_B = -0.05298011854
LIFT_C = 0.8829110762
LIFT_D = 0.4435068522
LIFT_K = 1.149604398


def shift_pairs(count, step):
    return [(i, (i + step) % count) for i in range(count)]


def extended_2(cells, sides, width):
    for axis, dim in sides:
        count = lax.axis_size(axis)
        size = cells.shape[dim]
        head = lax.slice_in_dim(cells, 0, width, axis=dim)
        tail = lax.slice_in_dim(cells, size - width, size, axis=dim)
        if count == 2:
            both = lax.ppermute(jnp.concatenate([tail, head], axis=dim), axis, shift_pairs(count, 1))
            left = lax.slice_in_dim(both, 0, width, axis=dim)
            right = lax.slice_in_dim(both, width, 2 * width, axis=dim)
        elif dim == cells.ndim - 1:
            def packed(piece):
                moved = jnp.moveaxis(piece, dim, 1)
                return moved.reshape(moved.shape[:2] + (-1,))

            def unpacked(flat):
                moved = flat.reshape((flat.shape[0], width) + cells.shape[1:dim])
                return jnp.moveaxis(moved, 1, dim)

            left = unpacked(lax.ppermute(packed(tail), axis, shift_pairs(count, 1)))
            right = unpacked(lax.ppermute(packed(head), axis, shift_pairs(count, -1)))
        else:
            left = lax.ppermute(tail, axis, shift_pairs(count, 1))
            right = lax.ppermute(head, axis, shift_pairs(count, -1))
        cells = jnp.concatenate([left, cells, right], axis=dim)
    return cells


def interpolation_matrix():
    nodes = np.array([-0.8611363116, -0.3399810436, 0.3399810436, 0.8611363116])
    targets = -0.75 + 0.5 * np.arange(4)
    table = np.ones((4, 4))
    for target_row in range(4):
        for node_col in range(4):
            for node_other in range(4):
                if node_other != node_col:
                    table[target_row, node_col] *= (targets[target_row] - nodes[node_other]) / (
                        nodes[node_col] - nodes[node_other]
                    )
    full_table = (
        table[:, None, None, :, None, None]
        * table[None, :, None, None, :, None]
        * table[None, None, :, None, None, :]
    ).reshape(64, 64)
    return jnp.asarray(full_table, dtype=jnp.float32)


def lift_table(length):
    extended = np.eye(length + 8)
    half_count = length // 2 + 4
    even_part = extended[0::2]
    odd_part = extended[1::2]
    odd_one = odd_part[0 : half_count - 1] + LIFT_A * (
        even_part[0 : half_count - 1] + even_part[1:half_count]
    )
    even_two = even_part[1 : half_count - 1] + LIFT_B * (
        odd_one[0 : half_count - 2] + odd_one[1 : half_count - 1]
    )
    odd_three = odd_one[1 : half_count - 2] + LIFT_C * (
        even_two[0 : half_count - 3] + even_two[1 : half_count - 2]
    )
    even_four = even_two[1 : half_count - 3] + LIFT_D * (
        odd_three[0 : half_count - 4] + odd_three[1 : half_count - 3]
    )
    joined = np.concatenate([even_four / LIFT_K, odd_three[1 : length // 2 + 1] * LIFT_K], 0)
    return jnp.asarray(joined, dtype=jnp.float32)


def apply_points(values, matrix):
    return jnp.einsum("qp,fpe->fqe", matrix, values, precision=lax.Precision.HIGHEST)


def to_cells(elements, size_x, size_y, size_z):
    blocks = elements.reshape(3, 4, 4, 4, size_x // 4, size_y // 4, size_z // 4)
    return blocks.transpose(0, 4, 1, 5, 2, 6, 3).reshape(3, size_x, size_y, size_z)


def lift_axis(extended, axis_dim, length):
    table = lift_table(length)
    if axis_dim == 1:
        return jnp.einsum("ab,fbyz->fayz", table, extended, precision=lax.Precision.HIGHEST)
    if axis_dim == 2:
        return jnp.einsum("ab,fxbz->fxaz", table, extended, precision=lax.Precision.HIGHEST)
    return jnp.einsum("fxyb,ab->fxya", extended, table, precision=lax.Precision.HIGHEST)


def spread_table():
    table = np.zeros((32, 4, 128), np.float32)
    for z_index in range(32):
        for c_index in range(4):
            table[z_index, c_index, 4 * z_index + c_index] = 1.0
    return jnp.asarray(table)


def rank_in_owner(target, groups):
    slots_here = target.shape[0]
    block = 128
    blocks = slots_here // block
    owner_ids = jnp.arange(groups, dtype=jnp.int32)
    onehot = (target[None, :] == owner_ids[:, None]).astype(jnp.bfloat16)
    onehot = onehot.reshape(groups, blocks, block)
    upper = (jnp.arange(block)[:, None] < jnp.arange(block)[None, :]).astype(jnp.bfloat16)
    within = jnp.einsum("obk,kj->obj", onehot, upper, preferred_element_type=jnp.float32)
    totals = jnp.sum(onehot.astype(jnp.float32), axis=2)
    block_upper = (jnp.arange(blocks)[:, None] < jnp.arange(blocks)[None, :]).astype(jnp.float32)
    offsets = jnp.dot(totals, block_upper, precision=lax.Precision.HIGHEST)
    counts = within + offsets[:, :, None]
    rank = jnp.sum(onehot.astype(jnp.float32) * counts, axis=0)
    return rank.reshape(slots_here).astype(jnp.int32)


def on_device(point_values, owner, slot, live_count):
    rows_x = lax.axis_size("gx")
    rows_y = lax.axis_size("gy")
    slab_size = rows_x * rows_y
    brick_elems = BX * BY * BZ // 64
    pair_capacity = 2 * brick_elems // slab_size
    slots_here = owner.shape[0]
    width = slab_size * pair_capacity
    flat_values = point_values.reshape(3 * 64, slots_here)
    position = jnp.arange(slots_here, dtype=jnp.int32)
    live = position < live_count[0]
    target = jnp.where(live, owner, slab_size)
    rank = rank_in_owner(target, slab_size)
    column = jnp.where(live, target * pair_capacity + rank, width)
    payload = jnp.concatenate([flat_values, (slot + 1).astype(jnp.float32)[None, :]], axis=0)
    send = jnp.zeros((3 * 64 + 1, width), jnp.float32).at[:, column].set(payload, mode="drop")
    halves = lax.all_to_all(
        send.reshape(3 * 64 + 1, rows_x, width // rows_x), "gx", split_axis=1, concat_axis=1, tiled=True
    )
    lanes = halves.reshape(3 * 64 + 1, rows_x, rows_y, pair_capacity).transpose(0, 2, 1, 3)
    recv = lax.all_to_all(
        lanes.reshape(3 * 64 + 1, rows_y, rows_x * pair_capacity), "gy", split_axis=1, concat_axis=1, tiled=True
    ).reshape(3 * 64 + 1, width)
    marks = recv[3 * 64].astype(jnp.int32)
    recv_slots = jnp.where(marks > 0, marks - 1, brick_elems)
    placed = (
        jnp.zeros((3 * 64, brick_elems), jnp.float32)
        .at[:, recv_slots]
        .set(recv[: 3 * 64], mode="drop")
    )
    matrix = interpolation_matrix()
    elements = jnp.einsum(
        "qp,fpe->fqe", matrix, placed.reshape(3, 64, brick_elems), precision=lax.Precision.HIGHEST
    )
    blocks = elements.reshape(3, 4, 4, 4, BX // 4, BY // 4, BZ // 4)
    coeffs = jnp.einsum(
        "fabcxyz,zcw->fxaybw", blocks, spread_table(), precision=lax.Precision.HIGHEST
    ).reshape(3, BX, BY, BZ)
    bands = []
    band = coeffs
    for level_index in range(LEVELS):
        size_x = BX >> level_index
        size_y = BY >> level_index
        size_z = BZ >> level_index
        band = band[:, :size_x, :size_y, :size_z]
        widened = extended_2(band, (("gx", 1),), 4)
        band = lift_axis(widened, 1, size_x)
        widened = extended_2(band, (("gy", 2),), 4)
        band = lift_axis(widened, 2, size_y)
        widened = extended_2(band, (("gz", 3),), 4)
        band = lift_axis(widened, 3, size_z)
        bands.append(band)
    result = bands[-1]
    for outer in reversed(bands[:-1]):
        padding = [(0, 0)] + [(0, outer.shape[d] - result.shape[d]) for d in range(1, 4)]
        inside = (
            (lax.broadcasted_iota(jnp.int32, outer.shape, 1) < result.shape[1])
            & (lax.broadcasted_iota(jnp.int32, outer.shape, 2) < result.shape[2])
            & (lax.broadcasted_iota(jnp.int32, outer.shape, 3) < result.shape[3])
        )
        result = jnp.where(inside, jnp.pad(result, padding), outer)
    return result


def solution(mesh):
    in_specs = (
        P(None, None, ("gx", "gy", "gz")),
        P(("gx", "gy", "gz")),
        P(("gx", "gy", "gz")),
        P(("gx", "gy", "gz")),
    )
    out_specs = P(None, "gx", "gy", "gz")
    return jax.shard_map(
        on_device, mesh=mesh, in_specs=in_specs, out_specs=out_specs, check_vma=False
    )
```

```python
import jax
import jax.numpy as jnp
import numpy as np
from jax import lax
from jax.sharding import PartitionSpec as P

BX = 32
BY = 32
BZ = 128
LEVELS = 3


LIFT_A = -1.586134342
LIFT_B = -0.05298011854
LIFT_C = 0.8829110762
LIFT_D = 0.4435068522
LIFT_K = 1.149604398


def shift_pairs(count, step):
    return [(i, (i + step) % count) for i in range(count)]


def extended_2(cells, sides, width):
    for axis, dim in sides:
        count = lax.axis_size(axis)
        size = cells.shape[dim]
        head = lax.slice_in_dim(cells, 0, width, axis=dim)
        tail = lax.slice_in_dim(cells, size - width, size, axis=dim)
        if count == 2:
            both = lax.ppermute(jnp.concatenate([tail, head], axis=dim), axis, shift_pairs(count, 1))
            left = lax.slice_in_dim(both, 0, width, axis=dim)
            right = lax.slice_in_dim(both, width, 2 * width, axis=dim)
        elif dim == cells.ndim - 1:
            def packed(piece):
                moved = jnp.moveaxis(piece, dim, 1)
                return moved.reshape(moved.shape[:2] + (-1,))

            def unpacked(flat):
                moved = flat.reshape((flat.shape[0], width) + cells.shape[1:dim])
                return jnp.moveaxis(moved, 1, dim)

            left = unpacked(lax.ppermute(packed(tail), axis, shift_pairs(count, 1)))
            right = unpacked(lax.ppermute(packed(head), axis, shift_pairs(count, -1)))
        else:
            left = lax.ppermute(tail, axis, shift_pairs(count, 1))
            right = lax.ppermute(head, axis, shift_pairs(count, -1))
        cells = jnp.concatenate([left, cells, right], axis=dim)
    return cells


def interpolation_matrix():
    nodes = np.array([-0.8611363116, -0.3399810436, 0.3399810436, 0.8611363116])
    targets = -0.75 + 0.5 * np.arange(4)
    table = np.ones((4, 4))
    for target_row in range(4):
        for node_col in range(4):
            for node_other in range(4):
                if node_other != node_col:
                    table[target_row, node_col] *= (targets[target_row] - nodes[node_other]) / (
                        nodes[node_col] - nodes[node_other]
                    )
    full_table = (
        table[:, None, None, :, None, None]
        * table[None, :, None, None, :, None]
        * table[None, None, :, None, None, :]
    ).reshape(64, 64)
    return jnp.asarray(full_table, dtype=jnp.float32)


def lift_table(length):
    extended = np.eye(length + 8)
    half_count = length // 2 + 4
    even_part = extended[0::2]
    odd_part = extended[1::2]
    odd_one = odd_part[0 : half_count - 1] + LIFT_A * (
        even_part[0 : half_count - 1] + even_part[1:half_count]
    )
    even_two = even_part[1 : half_count - 1] + LIFT_B * (
        odd_one[0 : half_count - 2] + odd_one[1 : half_count - 1]
    )
    odd_three = odd_one[1 : half_count - 2] + LIFT_C * (
        even_two[0 : half_count - 3] + even_two[1 : half_count - 2]
    )
    even_four = even_two[1 : half_count - 3] + LIFT_D * (
        odd_three[0 : half_count - 4] + odd_three[1 : half_count - 3]
    )
    joined = np.concatenate([even_four / LIFT_K, odd_three[1 : length // 2 + 1] * LIFT_K], 0)
    return jnp.asarray(joined, dtype=jnp.float32)


def apply_points(values, matrix):
    return jnp.einsum("qp,fpe->fqe", matrix, values, precision=lax.Precision.HIGHEST)


def to_cells(elements, size_x, size_y, size_z):
    blocks = elements.reshape(3, 4, 4, 4, size_x // 4, size_y // 4, size_z // 4)
    return blocks.transpose(0, 4, 1, 5, 2, 6, 3).reshape(3, size_x, size_y, size_z)


def lift_axis(extended, axis_dim, length):
    table = lift_table(length)
    if axis_dim == 1:
        return jnp.einsum("ab,fbyz->fayz", table, extended, precision=lax.Precision.HIGHEST)
    if axis_dim == 2:
        return jnp.einsum("ab,fxbz->fxaz", table, extended, precision=lax.Precision.HIGHEST)
    return jnp.einsum("fxyb,ab->fxya", extended, table, precision=lax.Precision.HIGHEST)


def spread_table():
    table = np.zeros((32, 4, 128), np.float32)
    for z_index in range(32):
        for c_index in range(4):
            table[z_index, c_index, 4 * z_index + c_index] = 1.0
    return jnp.asarray(table)


def rank_in_owner(target, groups):
    slots_here = target.shape[0]
    block = 128
    blocks = slots_here // block
    owner_ids = jnp.arange(groups, dtype=jnp.int32)
    onehot = (target[None, :] == owner_ids[:, None]).astype(jnp.bfloat16)
    onehot = onehot.reshape(groups, blocks, block)
    upper = (jnp.arange(block)[:, None] < jnp.arange(block)[None, :]).astype(jnp.bfloat16)
    within = jnp.einsum("obk,kj->obj", onehot, upper, preferred_element_type=jnp.float32)
    totals = jnp.sum(onehot.astype(jnp.float32), axis=2)
    block_upper = (jnp.arange(blocks)[:, None] < jnp.arange(blocks)[None, :]).astype(jnp.float32)
    offsets = jnp.dot(totals, block_upper, precision=lax.Precision.HIGHEST)
    counts = within + offsets[:, :, None]
    rank = jnp.sum(onehot.astype(jnp.float32) * counts, axis=0)
    return rank.reshape(slots_here).astype(jnp.int32)


def on_device(point_values, owner, slot, live_count):
    rows_x = lax.axis_size("gx")
    rows_y = lax.axis_size("gy")
    slab_size = rows_x * rows_y
    brick_elems = BX * BY * BZ // 64
    pair_capacity = 2 * brick_elems // slab_size
    slots_here = owner.shape[0]
    width = slab_size * pair_capacity
    flat_values = point_values.reshape(3 * 64, slots_here)
    position = jnp.arange(slots_here, dtype=jnp.int32)
    live = position < live_count[0]
    target = jnp.where(live, owner, slab_size)
    rank = rank_in_owner(target, slab_size)
    column = jnp.where(live, target * pair_capacity + rank, width)
    payload = jnp.concatenate([flat_values, (slot + 1).astype(jnp.float32)[None, :]], axis=0)
    send = jnp.zeros((3 * 64 + 1, width), jnp.float32).at[:, column].set(payload, mode="drop")
    recv = lax.all_to_all(send, ("gx", "gy"), split_axis=1, concat_axis=1, tiled=True)
    marks = recv[3 * 64].astype(jnp.int32)
    recv_slots = jnp.where(marks > 0, marks - 1, brick_elems)
    placed = (
        jnp.zeros((3 * 64, brick_elems), jnp.float32)
        .at[:, recv_slots]
        .set(recv[: 3 * 64], mode="drop")
    )
    matrix = interpolation_matrix()
    elements = jnp.einsum(
        "qp,fpe->fqe", matrix, placed.reshape(3, 64, brick_elems), precision=lax.Precision.HIGHEST
    )
    blocks = elements.reshape(3, 4, 4, 4, BX // 4, BY // 4, BZ // 4)
    high_part = lax.reduce_precision(blocks, exponent_bits=8, mantissa_bits=7)
    rest = blocks - high_part
    middle_part = lax.reduce_precision(rest, exponent_bits=8, mantissa_bits=7)
    low_part = rest - middle_part
    pieces = jnp.stack([high_part, middle_part, low_part], axis=0).astype(jnp.bfloat16)
    spread = jnp.broadcast_to(spread_table().astype(jnp.bfloat16)[None], (3,) + spread_table().shape)
    coeffs = jnp.einsum(
        "pfabcxyz,pzcw->fxaybw", pieces, spread, preferred_element_type=jnp.float32
    ).reshape(3, BX, BY, BZ)
    bands = []
    band = coeffs
    for level_index in range(LEVELS):
        size_x = BX >> level_index
        size_y = BY >> level_index
        size_z = BZ >> level_index
        band = band[:, :size_x, :size_y, :size_z]
        widened = extended_2(band, (("gx", 1),), 4)
        band = lift_axis(widened, 1, size_x)
        widened = extended_2(band, (("gy", 2),), 4)
        band = lift_axis(widened, 2, size_y)
        widened = extended_2(band, (("gz", 3),), 4)
        band = lift_axis(widened, 3, size_z)
        bands.append(band)
    result = bands[-1]
    for outer in reversed(bands[:-1]):
        padding = [(0, 0)] + [(0, outer.shape[d] - result.shape[d]) for d in range(1, 4)]
        inside = (
            (lax.broadcasted_iota(jnp.int32, outer.shape, 1) < result.shape[1])
            & (lax.broadcasted_iota(jnp.int32, outer.shape, 2) < result.shape[2])
            & (lax.broadcasted_iota(jnp.int32, outer.shape, 3) < result.shape[3])
        )
        result = jnp.where(inside, jnp.pad(result, padding), outer)
    return result


def solution(mesh):
    in_specs = (
        P(None, None, ("gx", "gy", "gz")),
        P(("gx", "gy", "gz")),
        P(("gx", "gy", "gz")),
        P(("gx", "gy", "gz")),
    )
    out_specs = P(None, "gx", "gy", "gz")
    return jax.shard_map(
        on_device, mesh=mesh, in_specs=in_specs, out_specs=out_specs, check_vma=False
    )
```

```python
import jax
import jax.numpy as jnp
import numpy as np
from jax import lax
from jax.sharding import PartitionSpec as P

BX = 32
BY = 32
BZ = 128
LEVELS = 3


LIFT_A = -1.586134342
LIFT_B = -0.05298011854
LIFT_C = 0.8829110762
LIFT_D = 0.4435068522
LIFT_K = 1.149604398


def shift_pairs(count, step):
    return [(i, (i + step) % count) for i in range(count)]


def extended_2(cells, sides, width):
    for axis, dim in sides:
        count = lax.axis_size(axis)
        size = cells.shape[dim]
        head = lax.slice_in_dim(cells, 0, width, axis=dim)
        tail = lax.slice_in_dim(cells, size - width, size, axis=dim)
        if count == 2:
            both = lax.ppermute(jnp.concatenate([tail, head], axis=dim), axis, shift_pairs(count, 1))
            left = lax.slice_in_dim(both, 0, width, axis=dim)
            right = lax.slice_in_dim(both, width, 2 * width, axis=dim)
        elif dim == cells.ndim - 1:
            def packed(piece):
                moved = jnp.moveaxis(piece, dim, 1)
                return moved.reshape(moved.shape[:2] + (-1,))

            def unpacked(flat):
                moved = flat.reshape((flat.shape[0], width) + cells.shape[1:dim])
                return jnp.moveaxis(moved, 1, dim)

            left = unpacked(lax.ppermute(packed(tail), axis, shift_pairs(count, 1)))
            right = unpacked(lax.ppermute(packed(head), axis, shift_pairs(count, -1)))
        else:
            left = lax.ppermute(tail, axis, shift_pairs(count, 1))
            right = lax.ppermute(head, axis, shift_pairs(count, -1))
        cells = jnp.concatenate([left, cells, right], axis=dim)
    return cells


def interpolation_matrix():
    nodes = np.array([-0.8611363116, -0.3399810436, 0.3399810436, 0.8611363116])
    targets = -0.75 + 0.5 * np.arange(4)
    table = np.ones((4, 4))
    for target_row in range(4):
        for node_col in range(4):
            for node_other in range(4):
                if node_other != node_col:
                    table[target_row, node_col] *= (targets[target_row] - nodes[node_other]) / (
                        nodes[node_col] - nodes[node_other]
                    )
    full_table = (
        table[:, None, None, :, None, None]
        * table[None, :, None, None, :, None]
        * table[None, None, :, None, None, :]
    ).reshape(64, 64)
    return jnp.asarray(full_table, dtype=jnp.float32)


def lift_table(length):
    extended = np.eye(length + 8)
    half_count = length // 2 + 4
    even_part = extended[0::2]
    odd_part = extended[1::2]
    odd_one = odd_part[0 : half_count - 1] + LIFT_A * (
        even_part[0 : half_count - 1] + even_part[1:half_count]
    )
    even_two = even_part[1 : half_count - 1] + LIFT_B * (
        odd_one[0 : half_count - 2] + odd_one[1 : half_count - 1]
    )
    odd_three = odd_one[1 : half_count - 2] + LIFT_C * (
        even_two[0 : half_count - 3] + even_two[1 : half_count - 2]
    )
    even_four = even_two[1 : half_count - 3] + LIFT_D * (
        odd_three[0 : half_count - 4] + odd_three[1 : half_count - 3]
    )
    joined = np.concatenate([even_four / LIFT_K, odd_three[1 : length // 2 + 1] * LIFT_K], 0)
    return jnp.asarray(joined, dtype=jnp.float32)


def apply_points(values, matrix):
    return jnp.einsum("qp,fpe->fqe", matrix, values, precision=lax.Precision.HIGHEST)


def to_cells(elements, size_x, size_y, size_z):
    blocks = elements.reshape(3, 4, 4, 4, size_x // 4, size_y // 4, size_z // 4)
    return blocks.transpose(0, 4, 1, 5, 2, 6, 3).reshape(3, size_x, size_y, size_z)


def lift_axis(extended, axis_dim, length):
    table = lift_table(length)
    if axis_dim == 1:
        return jnp.einsum("ab,fbyz->fayz", table, extended, precision=lax.Precision.HIGHEST)
    if axis_dim == 2:
        return jnp.einsum("ab,fxbz->fxaz", table, extended, precision=lax.Precision.HIGHEST)
    return jnp.einsum("fxyb,ab->fxya", extended, table, precision=lax.Precision.HIGHEST)


def spread_table():
    table = np.zeros((32, 4, 128), np.float32)
    for z_index in range(32):
        for c_index in range(4):
            table[z_index, c_index, 4 * z_index + c_index] = 1.0
    return jnp.asarray(table)


def rank_in_owner(target, groups):
    slots_here = target.shape[0]
    block = 128
    blocks = slots_here // block
    owner_ids = jnp.arange(groups, dtype=jnp.int32)
    onehot = (target[None, :] == owner_ids[:, None]).astype(jnp.bfloat16)
    onehot = onehot.reshape(groups, blocks, block)
    upper = (jnp.arange(block)[:, None] < jnp.arange(block)[None, :]).astype(jnp.bfloat16)
    within = jnp.einsum("obk,kj->obj", onehot, upper, preferred_element_type=jnp.float32)
    totals = jnp.sum(onehot.astype(jnp.float32), axis=2)
    block_upper = (jnp.arange(blocks)[:, None] < jnp.arange(blocks)[None, :]).astype(jnp.float32)
    offsets = jnp.dot(totals, block_upper, precision=lax.Precision.HIGHEST)
    counts = within + offsets[:, :, None]
    rank = jnp.sum(onehot.astype(jnp.float32) * counts, axis=0)
    return rank.reshape(slots_here).astype(jnp.int32)


def on_device(point_values, owner, slot, live_count):
    rows_x = lax.axis_size("gx")
    rows_y = lax.axis_size("gy")
    slab_size = rows_x * rows_y
    brick_elems = BX * BY * BZ // 64
    pair_capacity = 2 * brick_elems // slab_size
    slots_here = owner.shape[0]
    width = slab_size * pair_capacity
    flat_values = point_values.reshape(3 * 64, slots_here)
    position = jnp.arange(slots_here, dtype=jnp.int32)
    live = position < live_count[0]
    target = jnp.where(live, owner, slab_size)
    rank = rank_in_owner(target, slab_size)
    column = jnp.where(live, target * pair_capacity + rank, width + position)
    payload = jnp.concatenate([flat_values, (slot + 1).astype(jnp.float32)[None, :]], axis=0)
    send = (
        jnp.zeros((3 * 64 + 1, width), jnp.float32)
        .at[:, column]
        .set(payload, mode="drop", unique_indices=True)
    )
    recv = lax.all_to_all(send, ("gx", "gy"), split_axis=1, concat_axis=1, tiled=True)
    marks = recv[3 * 64].astype(jnp.int32)
    recv_slots = jnp.where(marks > 0, marks - 1, brick_elems + jnp.arange(width, dtype=jnp.int32))
    placed = (
        jnp.zeros((3 * 64, brick_elems), jnp.float32)
        .at[:, recv_slots]
        .set(recv[: 3 * 64], mode="drop", unique_indices=True)
    )
    matrix = interpolation_matrix()
    elements = jnp.einsum(
        "qp,fpe->fqe", matrix, placed.reshape(3, 64, brick_elems), precision=lax.Precision.HIGHEST
    )
    blocks = elements.reshape(3, 4, 4, 4, BX // 4, BY // 4, BZ // 4)
    coeffs = jnp.einsum(
        "fabcxyz,zcw->fxaybw", blocks, spread_table(), precision=lax.Precision.HIGHEST
    ).reshape(3, BX, BY, BZ)
    bands = []
    band = coeffs
    for level_index in range(LEVELS):
        size_x = BX >> level_index
        size_y = BY >> level_index
        size_z = BZ >> level_index
        band = band[:, :size_x, :size_y, :size_z]
        widened = extended_2(band, (("gx", 1),), 4)
        band = lift_axis(widened, 1, size_x)
        widened = extended_2(band, (("gy", 2),), 4)
        band = lift_axis(widened, 2, size_y)
        widened = extended_2(band, (("gz", 3),), 4)
        band = lift_axis(widened, 3, size_z)
        bands.append(band)
    result = bands[-1]
    for outer in reversed(bands[:-1]):
        padding = [(0, 0)] + [(0, outer.shape[d] - result.shape[d]) for d in range(1, 4)]
        inside = (
            (lax.broadcasted_iota(jnp.int32, outer.shape, 1) < result.shape[1])
            & (lax.broadcasted_iota(jnp.int32, outer.shape, 2) < result.shape[2])
            & (lax.broadcasted_iota(jnp.int32, outer.shape, 3) < result.shape[3])
        )
        result = jnp.where(inside, jnp.pad(result, padding), outer)
    return result


def solution(mesh):
    in_specs = (
        P(None, None, ("gx", "gy", "gz")),
        P(("gx", "gy", "gz")),
        P(("gx", "gy", "gz")),
        P(("gx", "gy", "gz")),
    )
    out_specs = P(None, "gx", "gy", "gz")
    return jax.shard_map(
        on_device, mesh=mesh, in_specs=in_specs, out_specs=out_specs, check_vma=False
    )
```

```python
import jax
import jax.numpy as jnp
import numpy as np
from jax import lax
from jax.sharding import PartitionSpec as P

BX = 32
BY = 32
BZ = 128
LEVELS = 3


LIFT_A = -1.586134342
LIFT_B = -0.05298011854
LIFT_C = 0.8829110762
LIFT_D = 0.4435068522
LIFT_K = 1.149604398


def shift_pairs(count, step):
    return [(i, (i + step) % count) for i in range(count)]


def extended_2(cells, sides, width):
    for axis, dim in sides:
        count = lax.axis_size(axis)
        size = cells.shape[dim]
        head = lax.slice_in_dim(cells, 0, width, axis=dim)
        tail = lax.slice_in_dim(cells, size - width, size, axis=dim)
        if count == 2:
            both = lax.ppermute(jnp.concatenate([tail, head], axis=dim), axis, shift_pairs(count, 1))
            left = lax.slice_in_dim(both, 0, width, axis=dim)
            right = lax.slice_in_dim(both, width, 2 * width, axis=dim)
        elif dim == cells.ndim - 1:
            def packed(piece):
                moved = jnp.moveaxis(piece, dim, 1)
                return moved.reshape(moved.shape[:2] + (-1,))

            def unpacked(flat):
                moved = flat.reshape((flat.shape[0], width) + cells.shape[1:dim])
                return jnp.moveaxis(moved, 1, dim)

            left = unpacked(lax.ppermute(packed(tail), axis, shift_pairs(count, 1)))
            right = unpacked(lax.ppermute(packed(head), axis, shift_pairs(count, -1)))
        else:
            left = lax.ppermute(tail, axis, shift_pairs(count, 1))
            right = lax.ppermute(head, axis, shift_pairs(count, -1))
        cells = jnp.concatenate([left, cells, right], axis=dim)
    return cells


def interpolation_matrix():
    nodes = np.array([-0.8611363116, -0.3399810436, 0.3399810436, 0.8611363116])
    targets = -0.75 + 0.5 * np.arange(4)
    table = np.ones((4, 4))
    for target_row in range(4):
        for node_col in range(4):
            for node_other in range(4):
                if node_other != node_col:
                    table[target_row, node_col] *= (targets[target_row] - nodes[node_other]) / (
                        nodes[node_col] - nodes[node_other]
                    )
    full_table = (
        table[:, None, None, :, None, None]
        * table[None, :, None, None, :, None]
        * table[None, None, :, None, None, :]
    ).reshape(64, 64)
    return jnp.asarray(full_table, dtype=jnp.float32)


def lift_table(length):
    extended = np.eye(length + 8)
    half_count = length // 2 + 4
    even_part = extended[0::2]
    odd_part = extended[1::2]
    odd_one = odd_part[0 : half_count - 1] + LIFT_A * (
        even_part[0 : half_count - 1] + even_part[1:half_count]
    )
    even_two = even_part[1 : half_count - 1] + LIFT_B * (
        odd_one[0 : half_count - 2] + odd_one[1 : half_count - 1]
    )
    odd_three = odd_one[1 : half_count - 2] + LIFT_C * (
        even_two[0 : half_count - 3] + even_two[1 : half_count - 2]
    )
    even_four = even_two[1 : half_count - 3] + LIFT_D * (
        odd_three[0 : half_count - 4] + odd_three[1 : half_count - 3]
    )
    joined = np.concatenate([even_four / LIFT_K, odd_three[1 : length // 2 + 1] * LIFT_K], 0)
    return jnp.asarray(joined, dtype=jnp.float32)


def apply_points(values, matrix):
    return jnp.einsum("qp,fpe->fqe", matrix, values, precision=lax.Precision.HIGHEST)


def to_cells(elements, size_x, size_y, size_z):
    blocks = elements.reshape(3, 4, 4, 4, size_x // 4, size_y // 4, size_z // 4)
    return blocks.transpose(0, 4, 1, 5, 2, 6, 3).reshape(3, size_x, size_y, size_z)


def lift_axis(extended, axis_dim, length):
    table = lift_table(length)
    if axis_dim == 1:
        return jnp.einsum("ab,fbyz->fayz", table, extended, precision=lax.Precision.HIGH)
    if axis_dim == 2:
        return jnp.einsum("ab,fxbz->fxaz", table, extended, precision=lax.Precision.HIGH)
    return jnp.einsum("fxyb,ab->fxya", extended, table, precision=lax.Precision.HIGH)


def spread_table():
    table = np.zeros((32, 4, 128), np.float32)
    for z_index in range(32):
        for c_index in range(4):
            table[z_index, c_index, 4 * z_index + c_index] = 1.0
    return jnp.asarray(table)


def rank_in_owner(target, groups):
    slots_here = target.shape[0]
    block = 128
    blocks = slots_here // block
    owner_ids = jnp.arange(groups, dtype=jnp.int32)
    onehot = (target[None, :] == owner_ids[:, None]).astype(jnp.bfloat16)
    onehot = onehot.reshape(groups, blocks, block)
    upper = (jnp.arange(block)[:, None] < jnp.arange(block)[None, :]).astype(jnp.bfloat16)
    within = jnp.einsum("obk,kj->obj", onehot, upper, preferred_element_type=jnp.float32)
    totals = jnp.sum(onehot.astype(jnp.float32), axis=2)
    block_upper = (jnp.arange(blocks)[:, None] < jnp.arange(blocks)[None, :]).astype(jnp.float32)
    offsets = jnp.dot(totals, block_upper, precision=lax.Precision.HIGHEST)
    counts = within + offsets[:, :, None]
    rank = jnp.sum(onehot.astype(jnp.float32) * counts, axis=0)
    return rank.reshape(slots_here).astype(jnp.int32)


def on_device(point_values, owner, slot, live_count):
    rows_x = lax.axis_size("gx")
    rows_y = lax.axis_size("gy")
    slab_size = rows_x * rows_y
    brick_elems = BX * BY * BZ // 64
    pair_capacity = 2 * brick_elems // slab_size
    slots_here = owner.shape[0]
    width = slab_size * pair_capacity
    flat_values = point_values.reshape(3 * 64, slots_here)
    position = jnp.arange(slots_here, dtype=jnp.int32)
    live = position < live_count[0]
    target = jnp.where(live, owner, slab_size)
    rank = rank_in_owner(target, slab_size)
    column = jnp.where(live, target * pair_capacity + rank, width)
    payload = jnp.concatenate([flat_values, (slot + 1).astype(jnp.float32)[None, :]], axis=0)
    send = jnp.zeros((3 * 64 + 1, width), jnp.float32).at[:, column].set(payload, mode="drop")
    recv = lax.all_to_all(send, ("gx", "gy"), split_axis=1, concat_axis=1, tiled=True)
    marks = recv[3 * 64].astype(jnp.int32)
    recv_slots = jnp.where(marks > 0, marks - 1, brick_elems)
    placed = (
        jnp.zeros((3 * 64, brick_elems), jnp.float32)
        .at[:, recv_slots]
        .set(recv[: 3 * 64], mode="drop")
    )
    matrix = interpolation_matrix()
    elements = jnp.einsum(
        "qp,fpe->fqe", matrix, placed.reshape(3, 64, brick_elems), precision=lax.Precision.HIGHEST
    )
    blocks = elements.reshape(3, 4, 4, 4, BX // 4, BY // 4, BZ // 4)
    coeffs = jnp.einsum(
        "fabcxyz,zcw->fxaybw", blocks, spread_table(), precision=lax.Precision.HIGHEST
    ).reshape(3, BX, BY, BZ)
    bands = []
    band = coeffs
    for level_index in range(LEVELS):
        size_x = BX >> level_index
        size_y = BY >> level_index
        size_z = BZ >> level_index
        band = band[:, :size_x, :size_y, :size_z]
        widened = extended_2(band, (("gx", 1),), 4)
        band = lift_axis(widened, 1, size_x)
        widened = extended_2(band, (("gy", 2),), 4)
        band = lift_axis(widened, 2, size_y)
        widened = extended_2(band, (("gz", 3),), 4)
        band = lift_axis(widened, 3, size_z)
        bands.append(band)
    result = bands[-1]
    for outer in reversed(bands[:-1]):
        padding = [(0, 0)] + [(0, outer.shape[d] - result.shape[d]) for d in range(1, 4)]
        inside = (
            (lax.broadcasted_iota(jnp.int32, outer.shape, 1) < result.shape[1])
            & (lax.broadcasted_iota(jnp.int32, outer.shape, 2) < result.shape[2])
            & (lax.broadcasted_iota(jnp.int32, outer.shape, 3) < result.shape[3])
        )
        result = jnp.where(inside, jnp.pad(result, padding), outer)
    return result


def solution(mesh):
    in_specs = (
        P(None, None, ("gx", "gy", "gz")),
        P(("gx", "gy", "gz")),
        P(("gx", "gy", "gz")),
        P(("gx", "gy", "gz")),
    )
    out_specs = P(None, "gx", "gy", "gz")
    return jax.shard_map(
        on_device, mesh=mesh, in_specs=in_specs, out_specs=out_specs, check_vma=False
    )
```

```python
import jax
import jax.numpy as jnp
import numpy as np
from jax import lax
from jax.sharding import PartitionSpec as P

BX = 32
BY = 32
BZ = 128
LEVELS = 3


LIFT_A = -1.586134342
LIFT_B = -0.05298011854
LIFT_C = 0.8829110762
LIFT_D = 0.4435068522
LIFT_K = 1.149604398


def shift_pairs(count, step):
    return [(i, (i + step) % count) for i in range(count)]


def extended_2(cells, sides, width):
    for axis, dim in sides:
        count = lax.axis_size(axis)
        size = cells.shape[dim]
        head = lax.slice_in_dim(cells, 0, width, axis=dim)
        tail = lax.slice_in_dim(cells, size - width, size, axis=dim)
        if count == 2:
            both = lax.ppermute(jnp.concatenate([tail, head], axis=dim), axis, shift_pairs(count, 1))
            left = lax.slice_in_dim(both, 0, width, axis=dim)
            right = lax.slice_in_dim(both, width, 2 * width, axis=dim)
        elif dim == cells.ndim - 1:
            def packed(piece):
                moved = jnp.moveaxis(piece, dim, 1)
                return moved.reshape(moved.shape[:2] + (-1,))

            def unpacked(flat):
                moved = flat.reshape((flat.shape[0], width) + cells.shape[1:dim])
                return jnp.moveaxis(moved, 1, dim)

            left = unpacked(lax.ppermute(packed(tail), axis, shift_pairs(count, 1)))
            right = unpacked(lax.ppermute(packed(head), axis, shift_pairs(count, -1)))
        else:
            left = lax.ppermute(tail, axis, shift_pairs(count, 1))
            right = lax.ppermute(head, axis, shift_pairs(count, -1))
        cells = jnp.concatenate([left, cells, right], axis=dim)
    return cells


def interpolation_matrix():
    nodes = np.array([-0.8611363116, -0.3399810436, 0.3399810436, 0.8611363116])
    targets = -0.75 + 0.5 * np.arange(4)
    table = np.ones((4, 4))
    for target_row in range(4):
        for node_col in range(4):
            for node_other in range(4):
                if node_other != node_col:
                    table[target_row, node_col] *= (targets[target_row] - nodes[node_other]) / (
                        nodes[node_col] - nodes[node_other]
                    )
    full_table = (
        table[:, None, None, :, None, None]
        * table[None, :, None, None, :, None]
        * table[None, None, :, None, None, :]
    ).reshape(64, 64)
    return jnp.asarray(full_table, dtype=jnp.float32)


def lift_table(length):
    extended = np.eye(length + 8)
    half_count = length // 2 + 4
    even_part = extended[0::2]
    odd_part = extended[1::2]
    odd_one = odd_part[0 : half_count - 1] + LIFT_A * (
        even_part[0 : half_count - 1] + even_part[1:half_count]
    )
    even_two = even_part[1 : half_count - 1] + LIFT_B * (
        odd_one[0 : half_count - 2] + odd_one[1 : half_count - 1]
    )
    odd_three = odd_one[1 : half_count - 2] + LIFT_C * (
        even_two[0 : half_count - 3] + even_two[1 : half_count - 2]
    )
    even_four = even_two[1 : half_count - 3] + LIFT_D * (
        odd_three[0 : half_count - 4] + odd_three[1 : half_count - 3]
    )
    joined = np.concatenate([even_four / LIFT_K, odd_three[1 : length // 2 + 1] * LIFT_K], 0)
    return jnp.asarray(joined, dtype=jnp.float32)


def apply_points(values, matrix):
    return jnp.einsum("qp,fpe->fqe", matrix, values, precision=lax.Precision.HIGHEST)


def to_cells(elements, size_x, size_y, size_z):
    blocks = elements.reshape(3, 4, 4, 4, size_x // 4, size_y // 4, size_z // 4)
    return blocks.transpose(0, 4, 1, 5, 2, 6, 3).reshape(3, size_x, size_y, size_z)


def lift_axis(extended, axis_dim, length, precision=lax.Precision.HIGHEST):
    table = lift_table(length)
    if axis_dim == 1:
        return jnp.einsum("ab,fbyz->fayz", table, extended, precision=precision)
    if axis_dim == 2:
        return jnp.einsum("ab,fxbz->fxaz", table, extended, precision=precision)
    return jnp.einsum("fxyb,ab->fxya", extended, table, precision=precision)


def spread_table():
    table = np.zeros((32, 4, 128), np.float32)
    for z_index in range(32):
        for c_index in range(4):
            table[z_index, c_index, 4 * z_index + c_index] = 1.0
    return jnp.asarray(table)


def rank_in_owner(target, groups):
    slots_here = target.shape[0]
    block = 128
    blocks = slots_here // block
    owner_ids = jnp.arange(groups, dtype=jnp.int32)
    onehot = (target[None, :] == owner_ids[:, None]).astype(jnp.bfloat16)
    onehot = onehot.reshape(groups, blocks, block)
    upper = (jnp.arange(block)[:, None] < jnp.arange(block)[None, :]).astype(jnp.bfloat16)
    within = jnp.einsum("obk,kj->obj", onehot, upper, preferred_element_type=jnp.float32)
    totals = jnp.sum(onehot.astype(jnp.float32), axis=2)
    block_upper = (jnp.arange(blocks)[:, None] < jnp.arange(blocks)[None, :]).astype(jnp.float32)
    offsets = jnp.dot(totals, block_upper, precision=lax.Precision.HIGHEST)
    counts = within + offsets[:, :, None]
    rank = jnp.sum(onehot.astype(jnp.float32) * counts, axis=0)
    return rank.reshape(slots_here).astype(jnp.int32)


def on_device(point_values, owner, slot, live_count):
    rows_x = lax.axis_size("gx")
    rows_y = lax.axis_size("gy")
    slab_size = rows_x * rows_y
    brick_elems = BX * BY * BZ // 64
    pair_capacity = 2 * brick_elems // slab_size
    slots_here = owner.shape[0]
    width = slab_size * pair_capacity
    flat_values = point_values.reshape(3 * 64, slots_here)
    position = jnp.arange(slots_here, dtype=jnp.int32)
    live = position < live_count[0]
    target = jnp.where(live, owner, slab_size)
    rank = rank_in_owner(target, slab_size)
    column = jnp.where(live, target * pair_capacity + rank, width)
    payload = jnp.concatenate([flat_values, (slot + 1).astype(jnp.float32)[None, :]], axis=0)
    send = jnp.zeros((3 * 64 + 1, width), jnp.float32).at[:, column].set(payload, mode="drop")
    recv = lax.all_to_all(send, ("gx", "gy"), split_axis=1, concat_axis=1, tiled=True)
    marks = recv[3 * 64].astype(jnp.int32)
    recv_slots = jnp.where(marks > 0, marks - 1, brick_elems)
    placed = (
        jnp.zeros((3 * 64, brick_elems), jnp.float32)
        .at[:, recv_slots]
        .set(recv[: 3 * 64], mode="drop")
    )
    matrix = interpolation_matrix()
    elements = jnp.einsum(
        "qp,fpe->fqe", matrix, placed.reshape(3, 64, brick_elems), precision=lax.Precision.HIGHEST
    )
    blocks = elements.reshape(3, 4, 4, 4, BX // 4, BY // 4, BZ // 4)
    coeffs = jnp.einsum(
        "fabcxyz,zcw->fxaybw", blocks, spread_table(), precision=lax.Precision.HIGHEST
    ).reshape(3, BX, BY, BZ)
    bands = []
    band = coeffs
    for level_index in range(LEVELS):
        size_x = BX >> level_index
        size_y = BY >> level_index
        size_z = BZ >> level_index
        band = band[:, :size_x, :size_y, :size_z]
        precision = lax.Precision.HIGH if level_index == 0 else lax.Precision.HIGHEST
        widened = extended_2(band, (("gx", 1),), 4)
        band = lift_axis(widened, 1, size_x, precision)
        widened = extended_2(band, (("gy", 2),), 4)
        band = lift_axis(widened, 2, size_y, precision)
        widened = extended_2(band, (("gz", 3),), 4)
        band = lift_axis(widened, 3, size_z, precision)
        bands.append(band)
    result = bands[-1]
    for outer in reversed(bands[:-1]):
        padding = [(0, 0)] + [(0, outer.shape[d] - result.shape[d]) for d in range(1, 4)]
        inside = (
            (lax.broadcasted_iota(jnp.int32, outer.shape, 1) < result.shape[1])
            & (lax.broadcasted_iota(jnp.int32, outer.shape, 2) < result.shape[2])
            & (lax.broadcasted_iota(jnp.int32, outer.shape, 3) < result.shape[3])
        )
        result = jnp.where(inside, jnp.pad(result, padding), outer)
    return result


def solution(mesh):
    in_specs = (
        P(None, None, ("gx", "gy", "gz")),
        P(("gx", "gy", "gz")),
        P(("gx", "gy", "gz")),
        P(("gx", "gy", "gz")),
    )
    out_specs = P(None, "gx", "gy", "gz")
    return jax.shard_map(
        on_device, mesh=mesh, in_specs=in_specs, out_specs=out_specs, check_vma=False
    )
```

```python
import jax
import jax.numpy as jnp
import numpy as np
from jax import lax
from jax.sharding import PartitionSpec as P

BX = 32
BY = 32
BZ = 128
LEVELS = 3


LIFT_A = -1.586134342
LIFT_B = -0.05298011854
LIFT_C = 0.8829110762
LIFT_D = 0.4435068522
LIFT_K = 1.149604398


def shift_pairs(count, step):
    return [(i, (i + step) % count) for i in range(count)]


def extended_2(cells, sides, width):
    for axis, dim in sides:
        count = lax.axis_size(axis)
        size = cells.shape[dim]
        head = lax.slice_in_dim(cells, 0, width, axis=dim)
        tail = lax.slice_in_dim(cells, size - width, size, axis=dim)
        if count == 2:
            both = lax.ppermute(jnp.concatenate([tail, head], axis=dim), axis, shift_pairs(count, 1))
            left = lax.slice_in_dim(both, 0, width, axis=dim)
            right = lax.slice_in_dim(both, width, 2 * width, axis=dim)
        elif dim == cells.ndim - 1:
            def packed(piece):
                moved = jnp.moveaxis(piece, dim, 1)
                return moved.reshape(moved.shape[:2] + (-1,))

            def unpacked(flat):
                moved = flat.reshape((flat.shape[0], width) + cells.shape[1:dim])
                return jnp.moveaxis(moved, 1, dim)

            left = unpacked(lax.ppermute(packed(tail), axis, shift_pairs(count, 1)))
            right = unpacked(lax.ppermute(packed(head), axis, shift_pairs(count, -1)))
        else:
            left = lax.ppermute(tail, axis, shift_pairs(count, 1))
            right = lax.ppermute(head, axis, shift_pairs(count, -1))
        cells = jnp.concatenate([left, cells, right], axis=dim)
    return cells


def interpolation_matrix():
    nodes = np.array([-0.8611363116, -0.3399810436, 0.3399810436, 0.8611363116])
    targets = -0.75 + 0.5 * np.arange(4)
    table = np.ones((4, 4))
    for target_row in range(4):
        for node_col in range(4):
            for node_other in range(4):
                if node_other != node_col:
                    table[target_row, node_col] *= (targets[target_row] - nodes[node_other]) / (
                        nodes[node_col] - nodes[node_other]
                    )
    full_table = (
        table[:, None, None, :, None, None]
        * table[None, :, None, None, :, None]
        * table[None, None, :, None, None, :]
    ).reshape(64, 64)
    return jnp.asarray(full_table, dtype=jnp.float32)


def lift_table(length):
    extended = np.eye(length + 8)
    half_count = length // 2 + 4
    even_part = extended[0::2]
    odd_part = extended[1::2]
    odd_one = odd_part[0 : half_count - 1] + LIFT_A * (
        even_part[0 : half_count - 1] + even_part[1:half_count]
    )
    even_two = even_part[1 : half_count - 1] + LIFT_B * (
        odd_one[0 : half_count - 2] + odd_one[1 : half_count - 1]
    )
    odd_three = odd_one[1 : half_count - 2] + LIFT_C * (
        even_two[0 : half_count - 3] + even_two[1 : half_count - 2]
    )
    even_four = even_two[1 : half_count - 3] + LIFT_D * (
        odd_three[0 : half_count - 4] + odd_three[1 : half_count - 3]
    )
    joined = np.concatenate([even_four / LIFT_K, odd_three[1 : length // 2 + 1] * LIFT_K], 0)
    return jnp.asarray(joined, dtype=jnp.float32)


def apply_points(values, matrix):
    return jnp.einsum("qp,fpe->fqe", matrix, values, precision=lax.Precision.HIGHEST)


def to_cells(elements, size_x, size_y, size_z):
    blocks = elements.reshape(3, 4, 4, 4, size_x // 4, size_y // 4, size_z // 4)
    return blocks.transpose(0, 4, 1, 5, 2, 6, 3).reshape(3, size_x, size_y, size_z)


def lift_axis(extended, axis_dim, length, precision=lax.Precision.HIGHEST):
    table = lift_table(length)
    if axis_dim == 1:
        return jnp.einsum("ab,fbyz->fayz", table, extended, precision=precision)
    if axis_dim == 2:
        return jnp.einsum("ab,fxbz->fxaz", table, extended, precision=precision)
    return jnp.einsum("fxyb,ab->fxya", extended, table, precision=precision)


def spread_table():
    table = np.zeros((32, 4, 128), np.float32)
    for z_index in range(32):
        for c_index in range(4):
            table[z_index, c_index, 4 * z_index + c_index] = 1.0
    return jnp.asarray(table)


def rank_in_owner(target, groups):
    slots_here = target.shape[0]
    block = 128
    blocks = slots_here // block
    owner_ids = jnp.arange(groups, dtype=jnp.int32)
    onehot = (target[None, :] == owner_ids[:, None]).astype(jnp.bfloat16)
    onehot = onehot.reshape(groups, blocks, block)
    upper = (jnp.arange(block)[:, None] < jnp.arange(block)[None, :]).astype(jnp.bfloat16)
    within = jnp.einsum("obk,kj->obj", onehot, upper, preferred_element_type=jnp.float32)
    totals = jnp.sum(onehot.astype(jnp.float32), axis=2)
    block_upper = (jnp.arange(blocks)[:, None] < jnp.arange(blocks)[None, :]).astype(jnp.float32)
    offsets = jnp.dot(totals, block_upper, precision=lax.Precision.HIGHEST)
    counts = within + offsets[:, :, None]
    rank = jnp.sum(onehot.astype(jnp.float32) * counts, axis=0)
    return rank.reshape(slots_here).astype(jnp.int32)


def on_device(point_values, owner, slot, live_count):
    rows_x = lax.axis_size("gx")
    rows_y = lax.axis_size("gy")
    slab_size = rows_x * rows_y
    brick_elems = BX * BY * BZ // 64
    pair_capacity = 2 * brick_elems // slab_size
    slots_here = owner.shape[0]
    width = slab_size * pair_capacity
    flat_values = point_values.reshape(3 * 64, slots_here)
    position = jnp.arange(slots_here, dtype=jnp.int32)
    live = position < live_count[0]
    target = jnp.where(live, owner, slab_size)
    rank = rank_in_owner(target, slab_size)
    column = jnp.where(live, target * pair_capacity + rank, width)
    payload = jnp.concatenate([flat_values, (slot + 1).astype(jnp.float32)[None, :]], axis=0)
    send = jnp.zeros((3 * 64 + 1, width), jnp.float32).at[:, column].set(payload, mode="drop")
    recv = lax.all_to_all(send, ("gx", "gy"), split_axis=1, concat_axis=1, tiled=True)
    marks = recv[3 * 64].astype(jnp.int32)
    recv_slots = jnp.where(marks > 0, marks - 1, brick_elems)
    placed = (
        jnp.zeros((3 * 64, brick_elems), jnp.float32)
        .at[:, recv_slots]
        .set(recv[: 3 * 64], mode="drop")
    )
    matrix = interpolation_matrix()
    elements = jnp.einsum(
        "qp,fpe->fqe", matrix, placed.reshape(3, 64, brick_elems), precision=lax.Precision.HIGHEST
    )
    blocks = elements.reshape(3, 4, 4, 4, BX // 4, BY // 4, BZ // 4)
    coeffs = jnp.einsum(
        "fabcxyz,zcw->fxaybw", blocks, spread_table(), precision=lax.Precision.HIGH
    ).reshape(3, BX, BY, BZ)
    bands = []
    band = coeffs
    for level_index in range(LEVELS):
        size_x = BX >> level_index
        size_y = BY >> level_index
        size_z = BZ >> level_index
        band = band[:, :size_x, :size_y, :size_z]
        precision = lax.Precision.HIGH if level_index == 0 else lax.Precision.HIGHEST
        widened = extended_2(band, (("gx", 1),), 4)
        band = lift_axis(widened, 1, size_x, precision)
        widened = extended_2(band, (("gy", 2),), 4)
        band = lift_axis(widened, 2, size_y, precision)
        widened = extended_2(band, (("gz", 3),), 4)
        band = lift_axis(widened, 3, size_z, precision)
        bands.append(band)
    result = bands[-1]
    for outer in reversed(bands[:-1]):
        padding = [(0, 0)] + [(0, outer.shape[d] - result.shape[d]) for d in range(1, 4)]
        inside = (
            (lax.broadcasted_iota(jnp.int32, outer.shape, 1) < result.shape[1])
            & (lax.broadcasted_iota(jnp.int32, outer.shape, 2) < result.shape[2])
            & (lax.broadcasted_iota(jnp.int32, outer.shape, 3) < result.shape[3])
        )
        result = jnp.where(inside, jnp.pad(result, padding), outer)
    return result


def solution(mesh):
    in_specs = (
        P(None, None, ("gx", "gy", "gz")),
        P(("gx", "gy", "gz")),
        P(("gx", "gy", "gz")),
        P(("gx", "gy", "gz")),
    )
    out_specs = P(None, "gx", "gy", "gz")
    return jax.shard_map(
        on_device, mesh=mesh, in_specs=in_specs, out_specs=out_specs, check_vma=False
    )
```

```python
import jax
import jax.numpy as jnp
import numpy as np
from jax import lax
from jax.sharding import PartitionSpec as P

BX = 32
BY = 32
BZ = 128
LEVELS = 3


LIFT_A = -1.586134342
LIFT_B = -0.05298011854
LIFT_C = 0.8829110762
LIFT_D = 0.4435068522
LIFT_K = 1.149604398


def shift_pairs(count, step):
    return [(i, (i + step) % count) for i in range(count)]


def extended_2(cells, sides, width):
    for axis, dim in sides:
        count = lax.axis_size(axis)
        size = cells.shape[dim]
        head = lax.slice_in_dim(cells, 0, width, axis=dim)
        tail = lax.slice_in_dim(cells, size - width, size, axis=dim)
        if count == 2:
            both = lax.ppermute(jnp.concatenate([tail, head], axis=dim), axis, shift_pairs(count, 1))
            left = lax.slice_in_dim(both, 0, width, axis=dim)
            right = lax.slice_in_dim(both, width, 2 * width, axis=dim)
        elif dim == cells.ndim - 1:
            def packed(piece):
                moved = jnp.moveaxis(piece, dim, 1)
                return moved.reshape(moved.shape[:2] + (-1,))

            def unpacked(flat):
                moved = flat.reshape((flat.shape[0], width) + cells.shape[1:dim])
                return jnp.moveaxis(moved, 1, dim)

            left = unpacked(lax.ppermute(packed(tail), axis, shift_pairs(count, 1)))
            right = unpacked(lax.ppermute(packed(head), axis, shift_pairs(count, -1)))
        else:
            left = lax.ppermute(tail, axis, shift_pairs(count, 1))
            right = lax.ppermute(head, axis, shift_pairs(count, -1))
        cells = jnp.concatenate([left, cells, right], axis=dim)
    return cells


def interpolation_matrix():
    nodes = np.array([-0.8611363116, -0.3399810436, 0.3399810436, 0.8611363116])
    targets = -0.75 + 0.5 * np.arange(4)
    table = np.ones((4, 4))
    for target_row in range(4):
        for node_col in range(4):
            for node_other in range(4):
                if node_other != node_col:
                    table[target_row, node_col] *= (targets[target_row] - nodes[node_other]) / (
                        nodes[node_col] - nodes[node_other]
                    )
    full_table = (
        table[:, None, None, :, None, None]
        * table[None, :, None, None, :, None]
        * table[None, None, :, None, None, :]
    ).reshape(64, 64)
    return jnp.asarray(full_table, dtype=jnp.float32)


def lift_table(length):
    extended = np.eye(length + 8)
    half_count = length // 2 + 4
    even_part = extended[0::2]
    odd_part = extended[1::2]
    odd_one = odd_part[0 : half_count - 1] + LIFT_A * (
        even_part[0 : half_count - 1] + even_part[1:half_count]
    )
    even_two = even_part[1 : half_count - 1] + LIFT_B * (
        odd_one[0 : half_count - 2] + odd_one[1 : half_count - 1]
    )
    odd_three = odd_one[1 : half_count - 2] + LIFT_C * (
        even_two[0 : half_count - 3] + even_two[1 : half_count - 2]
    )
    even_four = even_two[1 : half_count - 3] + LIFT_D * (
        odd_three[0 : half_count - 4] + odd_three[1 : half_count - 3]
    )
    joined = np.concatenate([even_four / LIFT_K, odd_three[1 : length // 2 + 1] * LIFT_K], 0)
    return jnp.asarray(joined, dtype=jnp.float32)


def apply_points(values, matrix):
    return jnp.einsum("qp,fpe->fqe", matrix, values, precision=lax.Precision.HIGHEST)


def to_cells(elements, size_x, size_y, size_z):
    blocks = elements.reshape(3, 4, 4, 4, size_x // 4, size_y // 4, size_z // 4)
    return blocks.transpose(0, 4, 1, 5, 2, 6, 3).reshape(3, size_x, size_y, size_z)


def lift_axis(extended, axis_dim, length, precision=lax.Precision.HIGHEST):
    table = lift_table(length)
    if axis_dim == 1:
        return jnp.einsum("ab,fbyz->fayz", table, extended, precision=precision)
    if axis_dim == 2:
        return jnp.einsum("ab,fxbz->fxaz", table, extended, precision=precision)
    return jnp.einsum("fxyb,ab->fxya", extended, table, precision=precision)


def spread_table():
    table = np.zeros((32, 4, 128), np.float32)
    for z_index in range(32):
        for c_index in range(4):
            table[z_index, c_index, 4 * z_index + c_index] = 1.0
    return jnp.asarray(table)


def rank_in_owner(target, groups):
    slots_here = target.shape[0]
    block = 128
    blocks = slots_here // block
    owner_ids = jnp.arange(groups, dtype=jnp.int32)
    onehot = (target[None, :] == owner_ids[:, None]).astype(jnp.bfloat16)
    onehot = onehot.reshape(groups, blocks, block)
    upper = (jnp.arange(block)[:, None] < jnp.arange(block)[None, :]).astype(jnp.bfloat16)
    within = jnp.einsum("obk,kj->obj", onehot, upper, preferred_element_type=jnp.float32)
    totals = jnp.sum(onehot.astype(jnp.float32), axis=2)
    block_upper = (jnp.arange(blocks)[:, None] < jnp.arange(blocks)[None, :]).astype(jnp.float32)
    offsets = jnp.dot(totals, block_upper, precision=lax.Precision.HIGHEST)
    counts = within + offsets[:, :, None]
    rank = jnp.sum(onehot.astype(jnp.float32) * counts, axis=0)
    return rank.reshape(slots_here).astype(jnp.int32)


def on_device(point_values, owner, slot, live_count):
    rows_x = lax.axis_size("gx")
    rows_y = lax.axis_size("gy")
    slab_size = rows_x * rows_y
    brick_elems = BX * BY * BZ // 64
    pair_capacity = 2 * brick_elems // slab_size
    slots_here = owner.shape[0]
    width = slab_size * pair_capacity
    flat_values = point_values.reshape(3 * 64, slots_here)
    position = jnp.arange(slots_here, dtype=jnp.int32)
    live = position < live_count[0]
    target = jnp.where(live, owner, slab_size)
    rank = rank_in_owner(target, slab_size)
    column = jnp.where(live, target * pair_capacity + rank, width)
    payload = jnp.concatenate([flat_values, (slot + 1).astype(jnp.float32)[None, :]], axis=0)
    send = jnp.zeros((3 * 64 + 1, width), jnp.float32).at[:, column].set(payload, mode="drop")
    recv = lax.all_to_all(send, ("gx", "gy"), split_axis=1, concat_axis=1, tiled=True)
    marks = recv[3 * 64].astype(jnp.int32)
    recv_slots = jnp.where(marks > 0, marks - 1, brick_elems)
    placed = (
        jnp.zeros((3 * 64, brick_elems), jnp.float32)
        .at[:, recv_slots]
        .set(recv[: 3 * 64], mode="drop")
    )
    matrix = interpolation_matrix()
    elements = jnp.einsum(
        "qp,fpxyz->fqxyz",
        matrix,
        placed.reshape(3, 64, BX // 4, BY // 4, BZ // 4),
        precision=lax.Precision.HIGHEST,
    )
    blocks = elements.reshape(3, 4, 4, 4, BX // 4, BY // 4, BZ // 4)
    coeffs = jnp.einsum(
        "fabcxyz,zcw->fxaybw", blocks, spread_table(), precision=lax.Precision.HIGH
    ).reshape(3, BX, BY, BZ)
    bands = []
    band = coeffs
    for level_index in range(LEVELS):
        size_x = BX >> level_index
        size_y = BY >> level_index
        size_z = BZ >> level_index
        band = band[:, :size_x, :size_y, :size_z]
        precision = lax.Precision.HIGH if level_index == 0 else lax.Precision.HIGHEST
        widened = extended_2(band, (("gx", 1),), 4)
        band = lift_axis(widened, 1, size_x, precision)
        widened = extended_2(band, (("gy", 2),), 4)
        band = lift_axis(widened, 2, size_y, precision)
        widened = extended_2(band, (("gz", 3),), 4)
        band = lift_axis(widened, 3, size_z, precision)
        bands.append(band)
    result = bands[-1]
    for outer in reversed(bands[:-1]):
        padding = [(0, 0)] + [(0, outer.shape[d] - result.shape[d]) for d in range(1, 4)]
        inside = (
            (lax.broadcasted_iota(jnp.int32, outer.shape, 1) < result.shape[1])
            & (lax.broadcasted_iota(jnp.int32, outer.shape, 2) < result.shape[2])
            & (lax.broadcasted_iota(jnp.int32, outer.shape, 3) < result.shape[3])
        )
        result = jnp.where(inside, jnp.pad(result, padding), outer)
    return result


def solution(mesh):
    in_specs = (
        P(None, None, ("gx", "gy", "gz")),
        P(("gx", "gy", "gz")),
        P(("gx", "gy", "gz")),
        P(("gx", "gy", "gz")),
    )
    out_specs = P(None, "gx", "gy", "gz")
    return jax.shard_map(
        on_device, mesh=mesh, in_specs=in_specs, out_specs=out_specs, check_vma=False
    )
```

```python
import jax
import jax.numpy as jnp
import numpy as np
from jax import lax
from jax.sharding import PartitionSpec as P

BX = 32
BY = 32
BZ = 128
LEVELS = 3


LIFT_A = -1.586134342
LIFT_B = -0.05298011854
LIFT_C = 0.8829110762
LIFT_D = 0.4435068522
LIFT_K = 1.149604398


def shift_pairs(count, step):
    return [(i, (i + step) % count) for i in range(count)]


def extended_2(cells, sides, width):
    for axis, dim in sides:
        count = lax.axis_size(axis)
        size = cells.shape[dim]
        head = lax.slice_in_dim(cells, 0, width, axis=dim)
        tail = lax.slice_in_dim(cells, size - width, size, axis=dim)
        if count == 2:
            both = lax.ppermute(jnp.concatenate([tail, head], axis=dim), axis, shift_pairs(count, 1))
            left = lax.slice_in_dim(both, 0, width, axis=dim)
            right = lax.slice_in_dim(both, width, 2 * width, axis=dim)
        elif dim == cells.ndim - 1:
            def packed(piece):
                moved = jnp.moveaxis(piece, dim, 1)
                return moved.reshape(moved.shape[:2] + (-1,))

            def unpacked(flat):
                moved = flat.reshape((flat.shape[0], width) + cells.shape[1:dim])
                return jnp.moveaxis(moved, 1, dim)

            left = unpacked(lax.ppermute(packed(tail), axis, shift_pairs(count, 1)))
            right = unpacked(lax.ppermute(packed(head), axis, shift_pairs(count, -1)))
        else:
            left = lax.ppermute(tail, axis, shift_pairs(count, 1))
            right = lax.ppermute(head, axis, shift_pairs(count, -1))
        cells = jnp.concatenate([left, cells, right], axis=dim)
    return cells


def interpolation_matrix():
    nodes = np.array([-0.8611363116, -0.3399810436, 0.3399810436, 0.8611363116])
    targets = -0.75 + 0.5 * np.arange(4)
    table = np.ones((4, 4))
    for target_row in range(4):
        for node_col in range(4):
            for node_other in range(4):
                if node_other != node_col:
                    table[target_row, node_col] *= (targets[target_row] - nodes[node_other]) / (
                        nodes[node_col] - nodes[node_other]
                    )
    full_table = (
        table[:, None, None, :, None, None]
        * table[None, :, None, None, :, None]
        * table[None, None, :, None, None, :]
    ).reshape(64, 64)
    return jnp.asarray(full_table, dtype=jnp.float32)


def lift_table(length):
    extended = np.eye(length + 8)
    half_count = length // 2 + 4
    even_part = extended[0::2]
    odd_part = extended[1::2]
    odd_one = odd_part[0 : half_count - 1] + LIFT_A * (
        even_part[0 : half_count - 1] + even_part[1:half_count]
    )
    even_two = even_part[1 : half_count - 1] + LIFT_B * (
        odd_one[0 : half_count - 2] + odd_one[1 : half_count - 1]
    )
    odd_three = odd_one[1 : half_count - 2] + LIFT_C * (
        even_two[0 : half_count - 3] + even_two[1 : half_count - 2]
    )
    even_four = even_two[1 : half_count - 3] + LIFT_D * (
        odd_three[0 : half_count - 4] + odd_three[1 : half_count - 3]
    )
    joined = np.concatenate([even_four / LIFT_K, odd_three[1 : length // 2 + 1] * LIFT_K], 0)
    return jnp.asarray(joined, dtype=jnp.float32)


def apply_points(values, matrix):
    return jnp.einsum("qp,fpe->fqe", matrix, values, precision=lax.Precision.HIGHEST)


def to_cells(elements, size_x, size_y, size_z):
    blocks = elements.reshape(3, 4, 4, 4, size_x // 4, size_y // 4, size_z // 4)
    return blocks.transpose(0, 4, 1, 5, 2, 6, 3).reshape(3, size_x, size_y, size_z)


def lift_axis(extended, axis_dim, length, precision=lax.Precision.HIGHEST):
    table = lift_table(length)
    if axis_dim == 1:
        return jnp.einsum("ab,fbyz->fayz", table, extended, precision=precision)
    if axis_dim == 2:
        return jnp.einsum("ab,fxbz->fxaz", table, extended, precision=precision)
    return jnp.einsum("fxyb,ab->fxya", extended, table, precision=precision)


def spread_table():
    table = np.zeros((32, 4, 128), np.float32)
    for z_index in range(32):
        for c_index in range(4):
            table[z_index, c_index, 4 * z_index + c_index] = 1.0
    return jnp.asarray(table)


def rank_in_owner(target, groups):
    slots_here = target.shape[0]
    block = 128
    blocks = slots_here // block
    owner_ids = jnp.arange(groups, dtype=jnp.int32)
    onehot = (target[None, :] == owner_ids[:, None]).astype(jnp.bfloat16)
    onehot = onehot.reshape(groups, blocks, block)
    upper = (jnp.arange(block)[:, None] < jnp.arange(block)[None, :]).astype(jnp.bfloat16)
    within = jnp.einsum("obk,kj->obj", onehot, upper, preferred_element_type=jnp.float32)
    totals = jnp.sum(onehot.astype(jnp.float32), axis=2)
    block_upper = (jnp.arange(blocks)[:, None] < jnp.arange(blocks)[None, :]).astype(jnp.float32)
    offsets = jnp.dot(totals, block_upper, precision=lax.Precision.HIGHEST)
    counts = within + offsets[:, :, None]
    rank = jnp.sum(onehot.astype(jnp.float32) * counts, axis=0)
    return rank.reshape(slots_here).astype(jnp.int32)


def on_device(point_values, owner, slot, live_count):
    rows_x = lax.axis_size("gx")
    rows_y = lax.axis_size("gy")
    slab_size = rows_x * rows_y
    brick_elems = BX * BY * BZ // 64
    pair_capacity = 2 * brick_elems // slab_size
    slots_here = owner.shape[0]
    width = slab_size * pair_capacity
    flat_values = point_values.reshape(3 * 64, slots_here)
    position = jnp.arange(slots_here, dtype=jnp.int32)
    live = position < live_count[0]
    target = jnp.where(live, owner, slab_size)
    rank = rank_in_owner(target, slab_size)
    column = jnp.where(live, target * pair_capacity + rank, width)
    payload = jnp.concatenate([flat_values, (slot + 1).astype(jnp.float32)[None, :]], axis=0)
    send = jnp.zeros((3 * 64 + 1, width), jnp.float32).at[:, column].set(payload, mode="drop")
    recv = lax.all_to_all(send, ("gx", "gy"), split_axis=1, concat_axis=1, tiled=True)
    marks = recv[3 * 64].astype(jnp.int32)
    recv_slots = jnp.where(marks > 0, marks - 1, brick_elems)
    placed = (
        jnp.zeros((3 * 64, brick_elems), jnp.float32)
        .at[:, recv_slots]
        .set(recv[: 3 * 64], mode="drop")
    )
    matrix = interpolation_matrix()
    elements = jnp.einsum(
        "qp,fpe->fqe", matrix, placed.reshape(3, 64, brick_elems), precision=lax.Precision.HIGHEST
    )
    blocks = elements.reshape(3, 4, 4, 4, BX // 4, BY // 4, BZ // 4)
    coeffs = jnp.einsum(
        "fabcxyz,zcw->fxaybw", blocks, spread_table(), precision=lax.Precision.HIGH
    ).reshape(3, BX, BY, BZ)
    bands = []
    band = coeffs
    for level_index in range(LEVELS):
        size_x = BX >> level_index
        size_y = BY >> level_index
        size_z = BZ >> level_index
        band = band[:, :size_x, :size_y, :size_z]
        precision = lax.Precision.HIGH if level_index == 0 else lax.Precision.HIGHEST
        widened = extended_2(band, (("gx", 1),), 4)
        band = lift_axis(widened, 1, size_x, precision)
        widened = extended_2(band, (("gy", 2),), 4)
        band = lift_axis(widened, 2, size_y, precision)
        widened = extended_2(band, (("gz", 3),), 4)
        band = lift_axis(widened, 3, size_z, precision)
        bands.append(band)
    result = bands[0]
    for inner in bands[1:]:
        padding = [(0, 0)] + [(0, result.shape[d] - inner.shape[d]) for d in range(1, 4)]
        inside = (
            (lax.broadcasted_iota(jnp.int32, result.shape, 1) < inner.shape[1])
            & (lax.broadcasted_iota(jnp.int32, result.shape, 2) < inner.shape[2])
            & (lax.broadcasted_iota(jnp.int32, result.shape, 3) < inner.shape[3])
        )
        result = jnp.where(inside, jnp.pad(inner, padding), result)
    return result


def solution(mesh):
    in_specs = (
        P(None, None, ("gx", "gy", "gz")),
        P(("gx", "gy", "gz")),
        P(("gx", "gy", "gz")),
        P(("gx", "gy", "gz")),
    )
    out_specs = P(None, "gx", "gy", "gz")
    return jax.shard_map(
        on_device, mesh=mesh, in_specs=in_specs, out_specs=out_specs, check_vma=False
    )
```
